128 devices in a mesh: dp: 8 (over x, core), tensor: 16 (over z, y).
Axes of the slice: x: 4, y: 4, z: 4, core: 2. Of those that a mesh axis runs over, the one named last changes fastest.
Arguments:
- hidden: bfloat16 [2048, 8192], P('dp', 'tensor'), may hold values from -170 to 170, as said below
- neighbour_ids: int32 [32, 2], P('dp'), may hold values from 0 to 255, as said below
- database: bfloat16 [256, 128, 8192], P('dp', None, 'tensor'), may hold values from -6 to 6
- w_query: bfloat16 [8192, 4096], P(None, 'tensor'), may hold values from -0.0625 to 0.0625
- w_key: bfloat16 [8192, 4096], P(None, 'tensor'), may hold values from -0.0625 to 0.0625
- w_value: bfloat16 [8192, 4096], P(None, 'tensor'), may hold values from -0.0625 to 0.0625
- w_out: bfloat16 [4096, 8192], P('tensor'), may hold values from -0.09375 to 0.09375
Outputs:
- mixed: bfloat16 [2048, 8192], P('dp', 'tensor')
The draws below stay inside these ranges and needn't reach their ends.
Inputs may be any that keep to these rules, and one draw needn't show every extreme that they name: `neighbour_ids`: database block b is held by index b // 32 of dp. Among the 8 neighbour ids of one sequence (the rows of one device), at most 4 belong to the same holder, and in every sequence exactly 4 do. `hidden`: hidden states may be large for some tokens.
All inputs are finite; a program needn't handle non-finite values.
Results may differ from the reference program's by a relative error of at most 0.02.
Values may be sent and summed in bfloat16 or wider, within the bound.
No kernel may reach another device: no remote copies, remote signals or barrier semaphores. Data moves between devices by JAX's collectives and lax.ppermute only.
A program may use at most 128 MiB of HBM per device.

```python
import jax
import jax.numpy as jnp
from jax import lax

D = 8192
HEADS = 32
HD = 128
GROUP = 64
RET = 128
NEIGH = 2
TOK_DEV = 256
DB_DEV = 32
TOKENS = 2048
BLOCKS = 256
N_DP = 8


def draw_hidden(key, part):
    first_key = jax.random.fold_in(key, 0)
    base_values = jnp.clip(jax.random.normal(first_key, (TOKENS, D), jnp.float32), -6.0, 6.0)
    return base_values.astype(jnp.bfloat16)


def draw_neighbour_ids(key, part):
    keys_list = jax.random.split(key, 5)
    dp_count = TOKENS // TOK_DEV
    per_reader = NEIGH * TOK_DEV // GROUP
    capacity = per_reader // 2
    base_owner = jax.random.randint(keys_list[0], (), 0, dp_count)
    hot_owner = (base_owner + jax.random.randint(keys_list[1], (dp_count,), 0, max(dp_count // 4, 1))) % dp_count
    other_owner = (hot_owner[:, None] + 1 + jax.random.randint(keys_list[2], (dp_count, per_reader - capacity), 0, dp_count - 1)) % dp_count
    owners = jnp.concatenate([jnp.broadcast_to(hot_owner[:, None], (dp_count, capacity)), other_owner], 1)
    order_keys = jax.random.split(keys_list[3], dp_count)
    orders = jax.vmap(lambda order_key: jax.random.permutation(order_key, per_reader))(order_keys)
    owners = jnp.take_along_axis(owners, orders, axis=1)
    local_index = jax.random.randint(keys_list[4], (dp_count, per_reader), 0, DB_DEV)
    block_ids = owners * DB_DEV + local_index
    return block_ids.reshape(TOKENS // GROUP, NEIGH).astype(jnp.int32)


def steps_of(stream_key, shape, cuts, low, largest):
    def one(dim, parts):
        heights = jax.random.uniform(jax.random.fold_in(jax.random.fold_in(stream_key, 6), dim), (parts,), jnp.float32, low / len(cuts), largest / len(cuts))
        return jnp.repeat(jnp.exp(heights), shape[dim] // parts).reshape((-1,) + (1,) * (len(shape) - dim - 1))

    level = one(*cuts[0])
    for cut in cuts[1:]:
        level = level * one(*cut)
    return level


def gaussian(own_key, extent, scale, limit, cuts=(), kind=jnp.bfloat16):
    entries = scale * jax.random.normal(own_key, extent, jnp.float32)
    if cuts:
        entries = entries * steps_of(own_key, extent, cuts, -0.22, 0.18)
    return jnp.clip(entries, -limit, limit).astype(kind)


def setup_inputs(seed: int = 0) -> dict:
    seeds = jax.random.split(jax.random.key(seed), 8)
    return {
        "hidden": draw_hidden(jax.random.fold_in(seeds[7], 71), 0),
        "neighbour_ids": draw_neighbour_ids(jax.random.fold_in(seeds[7], 71), 0),
        "database": gaussian(seeds[2], (BLOCKS, RET, D), 1.0, 6.0, ((0, 8), (2, 16))),
        "w_query": gaussian(seeds[3], (D, HEADS * HD), D ** -0.5, 0.0625, ((1, 16),)),
        "w_key": gaussian(seeds[4], (D, HEADS * HD), D ** -0.5, 0.0625, ((1, 16),)),
        "w_value": gaussian(seeds[5], (D, HEADS * HD), D ** -0.5, 0.0625, ((1, 16),)),
        "w_out": gaussian(seeds[6], (HEADS * HD, D), (HEADS * HD) ** -0.5, 0.09375, ((0, 16),)),
    }


def attend(query_rows, key_rows, value_rows, heads_count, group_len):
    tok_count, width = query_rows.shape
    groups = tok_count // group_len
    head_size = width // heads_count
    shifted = jnp.concatenate([query_rows[group_len - 1:], jnp.zeros((group_len - 1, width), jnp.bfloat16)], 0)
    shifted = shifted.reshape(groups, group_len, heads_count, head_size).astype(jnp.float32)
    key_block = key_rows.reshape(groups, -1, heads_count, head_size).astype(jnp.float32)
    value_block = value_rows.reshape(groups, -1, heads_count, head_size).astype(jnp.float32)
    scores = jnp.einsum('cqhd,ckhd->chqk', shifted, key_block) / jnp.sqrt(jnp.float32(head_size))
    top_score = lax.optimization_barrier(jnp.max(scores, axis=-1, keepdims=True))
    weights_raw = jnp.exp(scores - top_score)
    soft = (weights_raw / lax.optimization_barrier(jnp.sum(weights_raw, axis=-1, keepdims=True))).astype(jnp.bfloat16)
    blended = jnp.einsum('chqk,ckhd->cqhd', soft.astype(jnp.float32), value_block).astype(jnp.bfloat16)
    blended = blended.reshape(tok_count, width)
    return jnp.concatenate([jnp.zeros((group_len - 1, width), jnp.bfloat16), blended[:tok_count - group_len + 1]], 0)

def reference(hidden, neighbour_ids, database, w_query, w_key, w_value, w_out):
    query_rows = jnp.dot(hidden, w_query, preferred_element_type=jnp.float32).astype(jnp.bfloat16)
    shard_query = query_rows.reshape(N_DP, TOK_DEV, HEADS * HD)
    shard_ids = neighbour_ids.reshape(N_DP, NEIGH * TOK_DEV // GROUP)

    def one_shard(pair):
        query_part, id_part = pair
        gathered = jnp.take(database, id_part, axis=0).reshape(-1, D)
        key_rows = jnp.dot(gathered, w_key, preferred_element_type=jnp.float32).astype(jnp.bfloat16)
        value_rows = jnp.dot(gathered, w_value, preferred_element_type=jnp.float32).astype(jnp.bfloat16)
        return attend(query_part, key_rows, value_rows, HEADS, GROUP)
    contexts = lax.map(one_shard, (shard_query, shard_ids)).reshape(TOKENS, HEADS * HD)
    return jnp.dot(contexts, w_out, preferred_element_type=jnp.float32).astype(jnp.bfloat16)
```

```python
import jax
import jax.numpy as jnp
from jax import lax
from jax.sharding import PartitionSpec as P

HD = 128


def attend(query_rows, key_rows, value_rows, heads_count, group_len):
    tok_count, width = query_rows.shape
    groups = tok_count // group_len
    head_size = width // heads_count
    shifted = jnp.concatenate(
        [query_rows[group_len - 1 :], jnp.zeros((group_len - 1, width), jnp.bfloat16)], 0
    )
    shifted = shifted.reshape(groups, group_len, heads_count, head_size)
    key_block = key_rows.reshape(groups, -1, heads_count, head_size)
    value_block = value_rows.reshape(groups, -1, heads_count, head_size)
    scores = jnp.einsum(
        "cqhd,ckhd->chqk", shifted, key_block, preferred_element_type=jnp.float32
    ) / jnp.sqrt(jnp.float32(head_size))
    top_score = jnp.max(scores, axis=-1, keepdims=True)
    weights_raw = jnp.exp(scores - top_score)
    soft = (weights_raw / jnp.sum(weights_raw, axis=-1, keepdims=True)).astype(jnp.bfloat16)
    blended = jnp.einsum(
        "chqk,ckhd->cqhd", soft, value_block, preferred_element_type=jnp.float32
    ).astype(jnp.bfloat16)
    blended = blended.reshape(tok_count, width)
    return jnp.concatenate(
        [jnp.zeros((group_len - 1, width), jnp.bfloat16), blended[: tok_count - group_len + 1]], 0
    )


def shards(hidden, neighbour_ids, database, w_query, w_key, w_value, w_out):
    dp_count = lax.axis_size("dp")
    tok_rows = hidden.shape[0]
    group_count = neighbour_ids.shape[0]
    per_reader = group_count * neighbour_ids.shape[1]
    capacity = per_reader // 2
    db_count = database.shape[0]
    ret_len = database.shape[1]
    col_count = database.shape[2]
    head_cols = w_query.shape[1]
    heads_local = head_cols // HD
    query_sum = jnp.dot(
        lax.all_gather(hidden, "tensor", axis=1, tiled=True),
        w_query,
        preferred_element_type=jnp.float32,
    )
    query_rows = query_sum.astype(jnp.bfloat16)
    block_ids = neighbour_ids.reshape(per_reader)
    owners = block_ids // db_count
    earlier = jnp.arange(per_reader)[:, None] > jnp.arange(per_reader)[None, :]
    slot_rank = jnp.sum(((owners[:, None] == owners[None, :]) & earlier).astype(jnp.int32), 1)
    slot_range = jnp.arange(capacity, dtype=jnp.int32)
    local_index = block_ids % db_count
    owner_range = jnp.arange(dp_count, dtype=jnp.int32)
    slot_hit = (owners[:, None, None] == owner_range[None, :, None]) & (
        slot_rank[:, None, None] == slot_range[None, None, :]
    )
    request_table = jnp.sum(slot_hit.astype(jnp.int32) * local_index[:, None, None], 0)
    requested = lax.all_to_all(request_table, "dp", split_axis=0, concat_axis=0, tiled=True)
    outgoing = jnp.take(database, requested.reshape(-1), axis=0).reshape(
        dp_count, capacity, ret_len, col_count
    )
    arrived = lax.all_to_all(outgoing, "dp", split_axis=0, concat_axis=0, tiled=True)
    neighbour_rows = jnp.take(
        arrived.reshape(dp_count * capacity, ret_len, col_count),
        owners * capacity + slot_rank,
        axis=0,
    )
    assembled = lax.all_gather(neighbour_rows, "tensor", axis=2, tiled=True).reshape(
        per_reader * ret_len, -1
    )
    key_sum = jnp.dot(assembled, w_key, preferred_element_type=jnp.float32)
    value_sum = jnp.dot(assembled, w_value, preferred_element_type=jnp.float32)
    key_rows = key_sum.astype(jnp.bfloat16)
    value_rows = value_sum.astype(jnp.bfloat16)
    group_len = tok_rows // group_count
    context = attend(query_rows, key_rows, value_rows, heads_local, group_len)
    live = context[group_len - 1 :]
    live_rows = live.shape[0]
    tensor_count = lax.axis_size("tensor")
    partial_out = jnp.dot(live, w_out, preferred_element_type=jnp.float32).astype(jnp.bfloat16)
    spread = lax.all_to_all(
        partial_out.reshape(live_rows, tensor_count, -1), "tensor", split_axis=1, concat_axis=1, tiled=True
    )
    summed = jnp.sum(spread.astype(jnp.float32), axis=1).astype(jnp.bfloat16)
    return jnp.concatenate([jnp.zeros((group_len - 1, summed.shape[1]), jnp.bfloat16), summed], 0)


def solution(mesh):
    placed = (
        P("dp", "tensor"),
        P("dp", None),
        P("dp", None, "tensor"),
        P(None, "tensor"),
        P(None, "tensor"),
        P(None, "tensor"),
        P("tensor", None),
    )
    return jax.shard_map(
        shards, mesh=mesh, in_specs=placed, out_specs=P("dp", "tensor"), check_vma=False
    )
```

```python
import jax
import jax.numpy as jnp
from jax import lax
from jax.sharding import PartitionSpec as P

HD = 128


def attend(query_live, key_rows, value_rows, heads_count, group_len, groups):
    live_count, width = query_live.shape
    head_size = width // heads_count
    shifted = jnp.concatenate(
        [query_live, jnp.zeros((groups * group_len - live_count, width), jnp.bfloat16)], 0
    )
    shifted = shifted.reshape(groups, group_len, heads_count, head_size)
    key_block = key_rows.reshape(groups, -1, heads_count, head_size)
    value_block = value_rows.reshape(groups, -1, heads_count, head_size)
    scores = jnp.einsum(
        "cqhd,ckhd->chqk", shifted, key_block, preferred_element_type=jnp.float32
    ) / jnp.sqrt(jnp.float32(head_size))
    top_score = jnp.max(scores, axis=-1, keepdims=True)
    weights_raw = jnp.exp(scores - top_score)
    soft = (weights_raw / jnp.sum(weights_raw, axis=-1, keepdims=True)).astype(jnp.bfloat16)
    blended = jnp.einsum(
        "chqk,ckhd->cqhd", soft, value_block, preferred_element_type=jnp.float32
    ).astype(jnp.bfloat16)
    return blended.reshape(groups * group_len, width)[:live_count]


def shards(hidden, neighbour_ids, database, w_query, w_key, w_value, w_out):
    dp_count = lax.axis_size("dp")
    tok_rows = hidden.shape[0]
    group_count = neighbour_ids.shape[0]
    per_reader = group_count * neighbour_ids.shape[1]
    capacity = per_reader // 2
    db_count = database.shape[0]
    ret_len = database.shape[1]
    col_count = database.shape[2]
    head_cols = w_query.shape[1]
    heads_local = head_cols // HD
    tensor_count = lax.axis_size("tensor")
    group_len = tok_rows // group_count
    hidden_parts = lax.all_gather(hidden[group_len - 1 :], "tensor", axis=0, tiled=False)
    query_sum = jnp.einsum(
        "srf,sfc->rc",
        hidden_parts,
        w_query.reshape(tensor_count, -1, head_cols),
        preferred_element_type=jnp.float32,
    )
    query_rows = query_sum.astype(jnp.bfloat16)
    block_ids = neighbour_ids.reshape(per_reader)
    owners = block_ids // db_count
    earlier = jnp.arange(per_reader)[:, None] > jnp.arange(per_reader)[None, :]
    slot_rank = jnp.sum(((owners[:, None] == owners[None, :]) & earlier).astype(jnp.int32), 1)
    slot_range = jnp.arange(capacity, dtype=jnp.int32)
    local_index = block_ids % db_count
    owner_range = jnp.arange(dp_count, dtype=jnp.int32)
    slot_hit = (owners[:, None, None] == owner_range[None, :, None]) & (
        slot_rank[:, None, None] == slot_range[None, None, :]
    )
    request_table = jnp.sum(slot_hit.astype(jnp.int32) * local_index[:, None, None], 0)
    requested = lax.all_to_all(request_table, "dp", split_axis=0, concat_axis=0, tiled=True)
    outgoing = jnp.take(database, requested.reshape(-1), axis=0, mode="clip").reshape(
        dp_count, capacity, ret_len, col_count
    )
    arrived = lax.all_to_all(outgoing, "dp", split_axis=0, concat_axis=0, tiled=True)
    neighbour_rows = jnp.take(
        arrived.reshape(dp_count * capacity, ret_len, col_count),
        owners * capacity + slot_rank,
        axis=0,
        mode="clip",
    )
    assembled = lax.all_gather(neighbour_rows, "tensor", axis=2, tiled=True).reshape(
        per_reader * ret_len, -1
    )
    key_sum = jnp.dot(assembled, w_key, preferred_element_type=jnp.float32)
    value_sum = jnp.dot(assembled, w_value, preferred_element_type=jnp.float32)
    key_rows = key_sum.astype(jnp.bfloat16)
    value_rows = value_sum.astype(jnp.bfloat16)
    live = attend(query_rows, key_rows, value_rows, heads_local, group_len, group_count)
    live_rows = live.shape[0]
    partial_out = jnp.dot(live, w_out, preferred_element_type=jnp.float32).astype(jnp.bfloat16)
    spread = lax.all_to_all(
        partial_out.reshape(live_rows, tensor_count, -1), "tensor", split_axis=1, concat_axis=1, tiled=True
    )
    summed = jnp.sum(spread.astype(jnp.float32), axis=1).astype(jnp.bfloat16)
    return jnp.concatenate([jnp.zeros((group_len - 1, summed.shape[1]), jnp.bfloat16), summed], 0)


def solution(mesh):
    placed = (
        P("dp", "tensor"),
        P("dp", None),
        P("dp", None, "tensor"),
        P(None, "tensor"),
        P(None, "tensor"),
        P(None, "tensor"),
        P("tensor", None),
    )
    return jax.shard_map(
        shards, mesh=mesh, in_specs=placed, out_specs=P("dp", "tensor"), check_vma=False
    )
```

```python
import jax
import jax.numpy as jnp
from jax import lax
from jax.sharding import PartitionSpec as P

HD = 128


def attend(query_live, key_rows, value_rows, heads_count, group_len, groups):
    live_count, width = query_live.shape
    head_size = width // heads_count
    shifted = jnp.concatenate(
        [query_live, jnp.zeros((groups * group_len - live_count, width), jnp.bfloat16)], 0
    )
    shifted = shifted.reshape(groups, group_len, heads_count, head_size)
    key_block = key_rows.reshape(groups, -1, heads_count, head_size)
    value_block = value_rows.reshape(groups, -1, heads_count, head_size)
    scores = jnp.einsum(
        "cqhd,ckhd->chqk", shifted, key_block, preferred_element_type=jnp.float32
    ) / jnp.sqrt(jnp.float32(head_size))
    top_score = jnp.max(scores, axis=-1, keepdims=True)
    weights_raw = jnp.exp(scores - top_score)
    soft = (weights_raw / jnp.sum(weights_raw, axis=-1, keepdims=True)).astype(jnp.bfloat16)
    blended = jnp.einsum(
        "chqk,ckhd->cqhd", soft, value_block, preferred_element_type=jnp.float32
    ).astype(jnp.bfloat16)
    return blended.reshape(groups * group_len, width)[:live_count]


def last_token(query_row, tail_rows, w_key, w_value, heads_count):
    tensor_count = lax.axis_size("tensor")
    col_count = tail_rows.shape[-1]
    tail = tail_rows.reshape(-1, col_count)
    features = w_key.shape[0]
    head_size = query_row.shape[0] // heads_count
    exact = lax.Precision.HIGHEST
    spread_query = jnp.einsum(
        "fhd,hd->hf",
        w_key.reshape(features, heads_count, head_size),
        query_row.reshape(heads_count, head_size),
        preferred_element_type=jnp.float32,
    )
    own_query = lax.all_to_all(
        spread_query.reshape(heads_count, tensor_count, col_count),
        "tensor",
        split_axis=1,
        concat_axis=0,
        tiled=True,
    ).reshape(-1, col_count)
    partial_scores = jnp.einsum(
        "hf,kf->hk", own_query, tail, precision=exact, preferred_element_type=jnp.float32
    )
    all_scores = lax.all_to_all(
        jnp.broadcast_to(partial_scores[None], (tensor_count,) + partial_scores.shape),
        "tensor",
        split_axis=0,
        concat_axis=0,
        tiled=True,
    )
    scores = jnp.sum(all_scores, axis=0) / jnp.sqrt(jnp.float32(head_size))
    top_score = jnp.max(scores, axis=-1, keepdims=True)
    weights_raw = jnp.exp(scores - top_score)
    soft = (weights_raw / jnp.sum(weights_raw, axis=-1, keepdims=True)).astype(jnp.bfloat16)
    mixed_rows = jnp.einsum("hk,kf->hf", soft, tail, preferred_element_type=jnp.float32)
    own_rows = lax.all_to_all(
        mixed_rows.reshape(tensor_count, heads_count, col_count),
        "tensor",
        split_axis=0,
        concat_axis=0,
        tiled=True,
    )
    own_rows = jnp.transpose(own_rows, (1, 0, 2)).reshape(heads_count, features)
    context = jnp.einsum(
        "hf,fhd->hd",
        own_rows,
        w_value.reshape(features, heads_count, head_size),
        precision=exact,
        preferred_element_type=jnp.float32,
    )
    return context.astype(jnp.bfloat16).reshape(-1)


def shards(hidden, neighbour_ids, database, w_query, w_key, w_value, w_out):
    dp_count = lax.axis_size("dp")
    tok_rows = hidden.shape[0]
    group_count = neighbour_ids.shape[0]
    per_reader = group_count * neighbour_ids.shape[1]
    capacity = per_reader // 2
    db_count = database.shape[0]
    ret_len = database.shape[1]
    col_count = database.shape[2]
    head_cols = w_query.shape[1]
    heads_local = head_cols // HD
    tensor_count = lax.axis_size("tensor")
    group_len = tok_rows // group_count
    hidden_parts = lax.all_gather(hidden[group_len - 1 :], "tensor", axis=0, tiled=False)
    query_sum = jnp.einsum(
        "srf,sfc->rc",
        hidden_parts,
        w_query.reshape(tensor_count, -1, head_cols),
        preferred_element_type=jnp.float32,
    )
    query_rows = query_sum.astype(jnp.bfloat16)
    block_ids = neighbour_ids.reshape(per_reader)
    owners = block_ids // db_count
    earlier = jnp.arange(per_reader)[:, None] > jnp.arange(per_reader)[None, :]
    slot_rank = jnp.sum(((owners[:, None] == owners[None, :]) & earlier).astype(jnp.int32), 1)
    slot_range = jnp.arange(capacity, dtype=jnp.int32)
    local_index = block_ids % db_count
    owner_range = jnp.arange(dp_count, dtype=jnp.int32)
    slot_hit = (owners[:, None, None] == owner_range[None, :, None]) & (
        slot_rank[:, None, None] == slot_range[None, None, :]
    )
    request_table = jnp.sum(slot_hit.astype(jnp.int32) * local_index[:, None, None], 0)
    requested = lax.all_to_all(request_table, "dp", split_axis=0, concat_axis=0, tiled=True)
    outgoing = jnp.take(database, requested.reshape(-1), axis=0, mode="clip").reshape(
        dp_count, capacity, ret_len, col_count
    )
    arrived = lax.all_to_all(outgoing, "dp", split_axis=0, concat_axis=0, tiled=True)
    neighbour_rows = jnp.take(
        arrived.reshape(dp_count * capacity, ret_len, col_count),
        owners * capacity + slot_rank,
        axis=0,
        mode="clip",
    )
    main_rows = per_reader - 2
    main_parts = lax.all_gather(neighbour_rows[:main_rows], "tensor", axis=0, tiled=False)
    w_key_parts = w_key.reshape(tensor_count, col_count, head_cols)
    w_value_parts = w_value.reshape(tensor_count, col_count, head_cols)
    key_rows = jnp.einsum(
        "snkf,sfc->nkc", main_parts, w_key_parts, preferred_element_type=jnp.float32
    ).astype(jnp.bfloat16).reshape(main_rows * ret_len, head_cols)
    value_rows = jnp.einsum(
        "snkf,sfc->nkc", main_parts, w_value_parts, preferred_element_type=jnp.float32
    ).astype(jnp.bfloat16).reshape(main_rows * ret_len, head_cols)
    main_groups = main_rows // 2
    main_live = attend(
        query_rows[: main_groups * group_len], key_rows, value_rows, heads_local, group_len, main_groups
    )
    last_live = last_token(
        query_rows[main_groups * group_len], neighbour_rows[main_rows:], w_key, w_value, heads_local
    )
    live = jnp.concatenate([main_live, last_live[None]], 0)
    live_rows = live.shape[0]
    partial_out = jnp.dot(live, w_out, preferred_element_type=jnp.float32).astype(jnp.bfloat16)
    spread = lax.all_to_all(
        partial_out.reshape(live_rows, tensor_count, -1), "tensor", split_axis=1, concat_axis=1, tiled=True
    )
    summed = jnp.sum(spread.astype(jnp.float32), axis=1).astype(jnp.bfloat16)
    return jnp.concatenate([jnp.zeros((group_len - 1, summed.shape[1]), jnp.bfloat16), summed], 0)


def solution(mesh):
    placed = (
        P("dp", "tensor"),
        P("dp", None),
        P("dp", None, "tensor"),
        P(None, "tensor"),
        P(None, "tensor"),
        P(None, "tensor"),
        P("tensor", None),
    )
    return jax.shard_map(
        shards, mesh=mesh, in_specs=placed, out_specs=P("dp", "tensor"), check_vma=False
    )
```

```python
import jax
import jax.numpy as jnp
from jax import lax
from jax.sharding import PartitionSpec as P

HD = 128


def attend(query_live, key_rows, value_rows, heads_count, group_len, groups):
    live_count, width = query_live.shape
    head_size = width // heads_count
    shifted = jnp.concatenate(
        [query_live, jnp.zeros((groups * group_len - live_count, width), jnp.bfloat16)], 0
    )
    shifted = shifted.reshape(groups, group_len, heads_count, head_size)
    key_block = key_rows.reshape(groups, -1, heads_count, head_size)
    value_block = value_rows.reshape(groups, -1, heads_count, head_size)
    scores = jnp.einsum(
        "cqhd,ckhd->chqk", shifted, key_block, preferred_element_type=jnp.float32
    ) / jnp.sqrt(jnp.float32(head_size))
    top_score = jnp.max(scores, axis=-1, keepdims=True)
    weights_raw = jnp.exp(scores - top_score)
    soft = (weights_raw / jnp.sum(weights_raw, axis=-1, keepdims=True)).astype(jnp.bfloat16)
    blended = jnp.einsum(
        "chqk,ckhd->cqhd", soft, value_block, preferred_element_type=jnp.float32
    ).astype(jnp.bfloat16)
    return blended.reshape(groups * group_len, width)[:live_count]


def last_token(query_row, tail_rows, w_key, w_value, heads_count):
    tensor_count = lax.axis_size("tensor")
    col_count = tail_rows.shape[-1]
    tail = tail_rows.reshape(-1, col_count)
    features = w_key.shape[0]
    head_size = query_row.shape[0] // heads_count
    exact = lax.Precision.HIGHEST
    spread_query = jnp.einsum(
        "fhd,hd->hf",
        w_key.reshape(features, heads_count, head_size),
        query_row.reshape(heads_count, head_size),
        preferred_element_type=jnp.float32,
    )
    own_query = lax.all_to_all(
        spread_query.reshape(heads_count, tensor_count, col_count),
        "tensor",
        split_axis=1,
        concat_axis=0,
        tiled=True,
    ).reshape(-1, col_count)
    partial_scores = jnp.einsum(
        "hf,kf->hk", own_query, tail, precision=exact, preferred_element_type=jnp.float32
    )
    all_scores = lax.all_to_all(
        jnp.broadcast_to(partial_scores[None], (tensor_count,) + partial_scores.shape),
        "tensor",
        split_axis=0,
        concat_axis=0,
        tiled=True,
    )
    scores = jnp.sum(all_scores, axis=0) / jnp.sqrt(jnp.float32(head_size))
    top_score = jnp.max(scores, axis=-1, keepdims=True)
    weights_raw = jnp.exp(scores - top_score)
    soft = (weights_raw / jnp.sum(weights_raw, axis=-1, keepdims=True)).astype(jnp.bfloat16)
    mixed_rows = jnp.einsum("hk,kf->hf", soft, tail, preferred_element_type=jnp.float32)
    own_rows = lax.all_to_all(
        mixed_rows.reshape(tensor_count, heads_count, col_count),
        "tensor",
        split_axis=0,
        concat_axis=0,
        tiled=True,
    )
    own_rows = jnp.transpose(own_rows, (1, 0, 2)).reshape(heads_count, features)
    context = jnp.einsum(
        "hf,fhd->hd",
        own_rows,
        w_value.reshape(features, heads_count, head_size),
        precision=exact,
        preferred_element_type=jnp.float32,
    )
    return context.astype(jnp.bfloat16).reshape(-1)


def shards(hidden, neighbour_ids, database, w_query, w_key, w_value, w_out):
    dp_count = lax.axis_size("dp")
    tok_rows = hidden.shape[0]
    group_count = neighbour_ids.shape[0]
    per_reader = group_count * neighbour_ids.shape[1]
    capacity = per_reader // 2
    db_count = database.shape[0]
    ret_len = database.shape[1]
    col_count = database.shape[2]
    head_cols = w_query.shape[1]
    heads_local = head_cols // HD
    tensor_count = lax.axis_size("tensor")
    group_len = tok_rows // group_count
    hidden_parts = lax.all_gather(hidden[group_len - 1 :], "tensor", axis=0, tiled=False)
    query_sum = jnp.einsum(
        "srf,sfc->rc",
        hidden_parts,
        w_query.reshape(tensor_count, -1, head_cols),
        preferred_element_type=jnp.float32,
    )
    query_rows = query_sum.astype(jnp.bfloat16)
    block_ids = neighbour_ids.reshape(per_reader)
    owners = block_ids // db_count
    earlier = jnp.arange(per_reader)[:, None] > jnp.arange(per_reader)[None, :]
    slot_rank = jnp.sum(((owners[:, None] == owners[None, :]) & earlier).astype(jnp.int32), 1)
    slot_range = jnp.arange(capacity, dtype=jnp.int32)
    local_index = block_ids % db_count
    owner_range = jnp.arange(dp_count, dtype=jnp.int32)
    slot_hit = (owners[:, None, None] == owner_range[None, :, None]) & (
        slot_rank[:, None, None] == slot_range[None, None, :]
    )
    request_table = jnp.sum(slot_hit.astype(jnp.int32) * local_index[:, None, None], 0)
    requested = lax.all_to_all(request_table, "dp", split_axis=0, concat_axis=0, tiled=True)
    outgoing = jnp.take(database, requested.reshape(-1), axis=0, mode="clip").reshape(
        dp_count, capacity, ret_len, col_count
    )
    arrived = lax.all_to_all(outgoing, "dp", split_axis=0, concat_axis=0, tiled=True)
    neighbour_rows = jnp.take(
        arrived.reshape(dp_count * capacity, ret_len, col_count),
        owners * capacity + slot_rank,
        axis=0,
        mode="clip",
    )
    main_rows = per_reader - 2
    main_parts = lax.all_gather(neighbour_rows[:main_rows], "tensor", axis=0, tiled=False)
    w_key_parts = w_key.reshape(tensor_count, col_count, head_cols)
    w_value_parts = w_value.reshape(tensor_count, col_count, head_cols)
    w_both = jnp.concatenate([w_key_parts, w_value_parts], axis=2)
    both_rows = jnp.einsum(
        "snkf,sfc->nkc", main_parts, w_both, preferred_element_type=jnp.float32
    ).astype(jnp.bfloat16)
    key_rows = both_rows[..., :head_cols].reshape(main_rows * ret_len, head_cols)
    value_rows = both_rows[..., head_cols:].reshape(main_rows * ret_len, head_cols)
    main_groups = main_rows // 2
    main_live = attend(
        query_rows[: main_groups * group_len], key_rows, value_rows, heads_local, group_len, main_groups
    )
    last_live = last_token(
        query_rows[main_groups * group_len], neighbour_rows[main_rows:], w_key, w_value, heads_local
    )
    live = jnp.concatenate([main_live, last_live[None]], 0)
    live_rows = live.shape[0]
    partial_out = jnp.einsum(
        "rc,csf->srf",
        live,
        w_out.reshape(head_cols, tensor_count, -1),
        preferred_element_type=jnp.float32,
    ).astype(jnp.bfloat16)
    spread = lax.all_to_all(partial_out, "tensor", split_axis=0, concat_axis=0, tiled=True)
    summed = jnp.sum(spread.astype(jnp.float32), axis=0).astype(jnp.bfloat16)
    return jnp.concatenate([jnp.zeros((group_len - 1, summed.shape[1]), jnp.bfloat16), summed], 0)


def solution(mesh):
    placed = (
        P("dp", "tensor"),
        P("dp", None),
        P("dp", None, "tensor"),
        P(None, "tensor"),
        P(None, "tensor"),
        P(None, "tensor"),
        P("tensor", None),
    )
    return jax.shard_map(
        shards, mesh=mesh, in_specs=placed, out_specs=P("dp", "tensor"), check_vma=False
    )
```

```python
import jax
import jax.numpy as jnp
from jax import lax
from jax.sharding import PartitionSpec as P

HD = 128


def attend(query_live, key_rows, value_rows, heads_count, group_len, groups):
    live_count, width = query_live.shape
    head_size = width // heads_count
    shifted = jnp.concatenate(
        [query_live, jnp.zeros((groups * group_len - live_count, width), jnp.bfloat16)], 0
    )
    shifted = shifted.reshape(groups, group_len, heads_count, head_size)
    key_block = key_rows.reshape(groups, -1, heads_count, head_size)
    value_block = value_rows.reshape(groups, -1, heads_count, head_size)
    scores = jnp.einsum(
        "cqhd,ckhd->chqk", shifted, key_block, preferred_element_type=jnp.float32
    ) / jnp.sqrt(jnp.float32(head_size))
    top_score = jnp.max(scores, axis=-1, keepdims=True)
    weights_raw = jnp.exp(scores - top_score)
    soft = (weights_raw / jnp.sum(weights_raw, axis=-1, keepdims=True)).astype(jnp.bfloat16)
    blended = jnp.einsum(
        "chqk,ckhd->cqhd", soft, value_block, preferred_element_type=jnp.float32
    ).astype(jnp.bfloat16)
    return blended.reshape(groups * group_len, width)[:live_count]


def last_token(query_row, tail_rows, w_key, w_value, heads_count):
    tensor_count = lax.axis_size("tensor")
    col_count = tail_rows.shape[-1]
    tail = tail_rows.reshape(-1, col_count)
    features = w_key.shape[0]
    head_size = query_row.shape[0] // heads_count
    exact = lax.Precision.HIGHEST
    spread_query = jnp.einsum(
        "fhd,hd->hf",
        w_key.reshape(features, heads_count, head_size),
        query_row.reshape(heads_count, head_size),
        preferred_element_type=jnp.float32,
    )
    own_query = lax.all_to_all(
        spread_query.reshape(heads_count, tensor_count, col_count),
        "tensor",
        split_axis=1,
        concat_axis=0,
        tiled=True,
    ).reshape(-1, col_count)
    partial_scores = jnp.einsum(
        "hf,kf->hk", own_query, tail, precision=exact, preferred_element_type=jnp.float32
    )
    all_scores = lax.all_to_all(
        jnp.broadcast_to(partial_scores[None], (tensor_count,) + partial_scores.shape),
        "tensor",
        split_axis=0,
        concat_axis=0,
        tiled=True,
    )
    scores = jnp.sum(all_scores, axis=0) / jnp.sqrt(jnp.float32(head_size))
    top_score = jnp.max(scores, axis=-1, keepdims=True)
    weights_raw = jnp.exp(scores - top_score)
    soft = (weights_raw / jnp.sum(weights_raw, axis=-1, keepdims=True)).astype(jnp.bfloat16)
    mixed_rows = jnp.einsum("hk,kf->hf", soft, tail, preferred_element_type=jnp.float32)
    own_rows = lax.all_to_all(
        mixed_rows.reshape(tensor_count, heads_count, col_count),
        "tensor",
        split_axis=0,
        concat_axis=0,
        tiled=True,
    )
    own_rows = jnp.transpose(own_rows, (1, 0, 2)).reshape(heads_count, features)
    context = jnp.einsum(
        "hf,fhd->hd",
        own_rows,
        w_value.reshape(features, heads_count, head_size),
        precision=exact,
        preferred_element_type=jnp.float32,
    )
    return context.astype(jnp.bfloat16).reshape(-1)


def shards(hidden, neighbour_ids, database, w_query, w_key, w_value, w_out):
    dp_count = lax.axis_size("dp")
    tok_rows = hidden.shape[0]
    group_count = neighbour_ids.shape[0]
    per_reader = group_count * neighbour_ids.shape[1]
    capacity = per_reader // 2
    db_count = database.shape[0]
    ret_len = database.shape[1]
    col_count = database.shape[2]
    head_cols = w_query.shape[1]
    heads_local = head_cols // HD
    tensor_count = lax.axis_size("tensor")
    group_len = tok_rows // group_count
    hidden_parts = lax.all_gather(hidden[group_len - 1 :], "tensor", axis=0, tiled=False)
    query_sum = jnp.einsum(
        "srf,sfc->rc",
        hidden_parts,
        w_query.reshape(tensor_count, -1, head_cols),
        preferred_element_type=jnp.float32,
    )
    query_rows = query_sum.astype(jnp.bfloat16)
    block_ids = neighbour_ids.reshape(per_reader)
    owners = block_ids // db_count
    earlier = jnp.arange(per_reader)[:, None] > jnp.arange(per_reader)[None, :]
    slot_rank = jnp.sum(((owners[:, None] == owners[None, :]) & earlier).astype(jnp.int32), 1)
    slot_range = jnp.arange(capacity, dtype=jnp.int32)
    local_index = block_ids % db_count
    owner_range = jnp.arange(dp_count, dtype=jnp.int32)
    slot_hit = (owners[:, None, None] == owner_range[None, :, None]) & (
        slot_rank[:, None, None] == slot_range[None, None, :]
    )
    request_table = jnp.sum(slot_hit.astype(jnp.int32) * local_index[:, None, None], 0)
    requested = lax.all_to_all(request_table, "dp", split_axis=0, concat_axis=0, tiled=True)
    outgoing = jnp.take(database, requested.reshape(-1), axis=0, mode="clip").reshape(
        dp_count, capacity, ret_len, col_count
    )
    arrived = lax.all_to_all(outgoing, "dp", split_axis=0, concat_axis=0, tiled=True)
    arrived_rows = arrived.reshape(dp_count * capacity, ret_len, col_count)
    arrived_slot = owners * capacity + slot_rank
    main_rows = per_reader - 2
    head_rows = jnp.take(arrived_rows, arrived_slot[:main_rows], axis=0, mode="clip")
    tail_rows = jnp.take(arrived_rows, arrived_slot[main_rows:], axis=0, mode="clip")
    main_parts = lax.all_gather(head_rows, "tensor", axis=0, tiled=False)
    w_key_parts = w_key.reshape(tensor_count, col_count, head_cols)
    w_value_parts = w_value.reshape(tensor_count, col_count, head_cols)
    w_both = lax.optimization_barrier(jnp.concatenate([w_key_parts, w_value_parts], axis=2))
    both_rows = jnp.einsum(
        "snkf,sfc->nkc", main_parts, w_both, preferred_element_type=jnp.float32
    ).astype(jnp.bfloat16)
    key_rows = both_rows[..., :head_cols].reshape(main_rows * ret_len, head_cols)
    value_rows = both_rows[..., head_cols:].reshape(main_rows * ret_len, head_cols)
    main_groups = main_rows // 2
    main_live = attend(
        query_rows[: main_groups * group_len], key_rows, value_rows, heads_local, group_len, main_groups
    )
    last_live = last_token(
        query_rows[main_groups * group_len], tail_rows, w_key, w_value, heads_local
    )
    live = jnp.concatenate([main_live, last_live[None]], 0)
    live_rows = live.shape[0]
    partial_out = jnp.einsum(
        "rc,csf->srf",
        live,
        w_out.reshape(head_cols, tensor_count, -1),
        preferred_element_type=jnp.float32,
    ).astype(jnp.bfloat16)
    spread = lax.all_to_all(partial_out, "tensor", split_axis=0, concat_axis=0, tiled=True)
    summed = jnp.sum(spread.astype(jnp.float32), axis=0).astype(jnp.bfloat16)
    return jnp.concatenate([jnp.zeros((group_len - 1, summed.shape[1]), jnp.bfloat16), summed], 0)


def solution(mesh):
    placed = (
        P("dp", "tensor"),
        P("dp", None),
        P("dp", None, "tensor"),
        P(None, "tensor"),
        P(None, "tensor"),
        P(None, "tensor"),
        P("tensor", None),
    )
    return jax.shard_map(
        shards, mesh=mesh, in_specs=placed, out_specs=P("dp", "tensor"), check_vma=False
    )
```

```python
import jax
import jax.numpy as jnp
from jax import lax
from jax.sharding import PartitionSpec as P

HD = 128


def attend(query_live, key_rows, value_rows, heads_count, group_len, groups):
    live_count, width = query_live.shape
    head_size = width // heads_count
    shifted = jnp.concatenate(
        [query_live, jnp.zeros((groups * group_len - live_count, width), jnp.bfloat16)], 0
    )
    shifted = shifted.reshape(groups, group_len, heads_count, head_size)
    key_block = key_rows.reshape(groups, -1, heads_count, head_size)
    value_block = value_rows.reshape(groups, -1, heads_count, head_size)
    scores = jnp.einsum(
        "cqhd,ckhd->chqk", shifted, key_block, preferred_element_type=jnp.float32
    ) / jnp.sqrt(jnp.float32(head_size))
    top_score = jnp.max(scores, axis=-1, keepdims=True)
    weights_raw = jnp.exp(scores - top_score)
    soft = (weights_raw / jnp.sum(weights_raw, axis=-1, keepdims=True)).astype(jnp.bfloat16)
    blended = jnp.einsum(
        "chqk,ckhd->cqhd", soft, value_block, preferred_element_type=jnp.float32
    ).astype(jnp.bfloat16)
    return blended.reshape(groups * group_len, width)[:live_count]


def last_token(query_row, tail_rows, w_key, w_value, heads_count):
    tensor_count = lax.axis_size("tensor")
    col_count = tail_rows.shape[-1]
    tail = tail_rows.reshape(-1, col_count)
    features = w_key.shape[0]
    head_size = query_row.shape[0] // heads_count
    exact = lax.Precision.HIGHEST
    spread_query = jnp.einsum(
        "fhd,hd->hf",
        w_key.reshape(features, heads_count, head_size),
        query_row.reshape(heads_count, head_size),
        preferred_element_type=jnp.float32,
    )
    own_query = lax.all_to_all(
        spread_query.reshape(heads_count, tensor_count, col_count),
        "tensor",
        split_axis=1,
        concat_axis=0,
        tiled=True,
    ).reshape(-1, col_count)
    partial_scores = jnp.einsum(
        "hf,kf->hk", own_query, tail, precision=exact, preferred_element_type=jnp.float32
    )
    all_scores = lax.all_to_all(
        jnp.broadcast_to(partial_scores[None], (tensor_count,) + partial_scores.shape),
        "tensor",
        split_axis=0,
        concat_axis=0,
        tiled=True,
    )
    scores = jnp.sum(all_scores, axis=0) / jnp.sqrt(jnp.float32(head_size))
    top_score = jnp.max(scores, axis=-1, keepdims=True)
    weights_raw = jnp.exp(scores - top_score)
    soft = (weights_raw / jnp.sum(weights_raw, axis=-1, keepdims=True)).astype(jnp.bfloat16)
    mixed_rows = jnp.einsum("hk,kf->hf", soft, tail, preferred_element_type=jnp.float32)
    own_rows = lax.all_to_all(
        mixed_rows.reshape(tensor_count, heads_count, col_count),
        "tensor",
        split_axis=0,
        concat_axis=0,
        tiled=True,
    )
    own_rows = jnp.transpose(own_rows, (1, 0, 2)).reshape(heads_count, features)
    context = jnp.einsum(
        "hf,fhd->hd",
        own_rows,
        w_value.reshape(features, heads_count, head_size),
        precision=exact,
        preferred_element_type=jnp.float32,
    )
    return context.astype(jnp.bfloat16).reshape(-1)


def shards(hidden, neighbour_ids, database, w_query, w_key, w_value, w_out):
    dp_count = lax.axis_size("dp")
    tok_rows = hidden.shape[0]
    group_count = neighbour_ids.shape[0]
    per_reader = group_count * neighbour_ids.shape[1]
    capacity = per_reader // 2
    db_count = database.shape[0]
    ret_len = database.shape[1]
    col_count = database.shape[2]
    head_cols = w_query.shape[1]
    heads_local = head_cols // HD
    tensor_count = lax.axis_size("tensor")
    group_len = tok_rows // group_count
    hidden_parts = lax.all_gather(hidden[group_len - 1 :], "tensor", axis=0, tiled=False)
    query_sum = jnp.einsum(
        "srf,sfc->rc",
        hidden_parts,
        w_query.reshape(tensor_count, -1, head_cols),
        preferred_element_type=jnp.float32,
    )
    query_rows = query_sum.astype(jnp.bfloat16)
    block_ids = neighbour_ids.reshape(per_reader)
    owners = block_ids // db_count
    earlier = jnp.arange(per_reader)[:, None] > jnp.arange(per_reader)[None, :]
    slot_rank = jnp.sum(((owners[:, None] == owners[None, :]) & earlier).astype(jnp.int32), 1)
    slot_range = jnp.arange(capacity, dtype=jnp.int32)
    local_index = block_ids % db_count
    owner_range = jnp.arange(dp_count, dtype=jnp.int32)
    slot_hit = (owners[:, None, None] == owner_range[None, :, None]) & (
        slot_rank[:, None, None] == slot_range[None, None, :]
    )
    request_table = jnp.sum(slot_hit.astype(jnp.int32) * local_index[:, None, None], 0)
    requested = lax.all_to_all(request_table, "dp", split_axis=0, concat_axis=0, tiled=True)
    outgoing = jnp.take(database, requested.reshape(-1), axis=0, mode="clip").reshape(
        dp_count, capacity, ret_len, col_count
    )
    arrived = lax.all_to_all(outgoing, "dp", split_axis=0, concat_axis=0, tiled=True)
    arrived_rows = arrived.reshape(dp_count * capacity, ret_len, col_count)
    arrived_slot = owners * capacity + slot_rank
    main_rows = per_reader - 2
    head_rows = jnp.take(arrived_rows, arrived_slot[:main_rows], axis=0, mode="clip")
    tail_rows = jnp.take(arrived_rows, arrived_slot[main_rows:], axis=0, mode="clip")
    w_key_parts = w_key.reshape(tensor_count, col_count, head_cols)
    w_value_parts = w_value.reshape(tensor_count, col_count, head_cols)
    w_both = lax.optimization_barrier(jnp.concatenate([w_key_parts, w_value_parts], axis=2))
    w_out_parts = w_out.reshape(head_cols, tensor_count, -1)
    last_live = last_token(
        query_rows[(main_rows // 2) * group_len], tail_rows, w_key, w_value, heads_local
    )

    def stage(rows, first_group, extra):
        stage_rows = rows.shape[0]
        parts = lax.all_gather(rows, "tensor", axis=0, tiled=False)
        both_rows = jnp.einsum(
            "snkf,sfc->nkc", parts, w_both, preferred_element_type=jnp.float32
        ).astype(jnp.bfloat16)
        key_rows = both_rows[..., :head_cols].reshape(stage_rows * ret_len, head_cols)
        value_rows = both_rows[..., head_cols:].reshape(stage_rows * ret_len, head_cols)
        groups = stage_rows // 2
        context = attend(
            query_rows[first_group * group_len : (first_group + groups) * group_len],
            key_rows,
            value_rows,
            heads_local,
            group_len,
            groups,
        )
        if extra is not None:
            context = jnp.concatenate([context, extra[None]], 0)
        partial_out = jnp.einsum(
            "rc,csf->srf", context, w_out_parts, preferred_element_type=jnp.float32
        ).astype(jnp.bfloat16)
        spread = lax.all_to_all(partial_out, "tensor", split_axis=0, concat_axis=0, tiled=True)
        return jnp.sum(spread.astype(jnp.float32), axis=0).astype(jnp.bfloat16)

    first_rows = ((main_rows // 2 + 1) // 2) * 2
    second_sum = stage(head_rows[first_rows:], first_rows // 2, last_live)
    first_sum = stage(head_rows[:first_rows], 0, None)
    summed = jnp.concatenate([first_sum, second_sum], 0)
    return jnp.concatenate([jnp.zeros((group_len - 1, summed.shape[1]), jnp.bfloat16), summed], 0)


def solution(mesh):
    placed = (
        P("dp", "tensor"),
        P("dp", None),
        P("dp", None, "tensor"),
        P(None, "tensor"),
        P(None, "tensor"),
        P(None, "tensor"),
        P("tensor", None),
    )
    return jax.shard_map(
        shards, mesh=mesh, in_specs=placed, out_specs=P("dp", "tensor"), check_vma=False
    )
```

```python
import jax
import jax.numpy as jnp
from jax import lax
from jax.sharding import PartitionSpec as P
from jax.experimental import pallas as pl
from jax.experimental.pallas import tpu as pltpu

HD = 128


def attend(query_live, key_rows, value_rows, heads_count, group_len, groups):
    live_count, width = query_live.shape
    head_size = width // heads_count
    shifted = jnp.concatenate(
        [query_live, jnp.zeros((groups * group_len - live_count, width), jnp.bfloat16)], 0
    )
    shifted = shifted.reshape(groups, group_len, heads_count, head_size)
    key_block = key_rows.reshape(groups, -1, heads_count, head_size)
    value_block = value_rows.reshape(groups, -1, heads_count, head_size)
    scores = jnp.einsum(
        "cqhd,ckhd->chqk", shifted, key_block, preferred_element_type=jnp.float32
    ) / jnp.sqrt(jnp.float32(head_size))
    top_score = jnp.max(scores, axis=-1, keepdims=True)
    weights_raw = jnp.exp(scores - top_score)
    soft = (weights_raw / jnp.sum(weights_raw, axis=-1, keepdims=True)).astype(jnp.bfloat16)
    blended = jnp.einsum(
        "chqk,ckhd->cqhd", soft, value_block, preferred_element_type=jnp.float32
    ).astype(jnp.bfloat16)
    return blended.reshape(groups * group_len, width)[:live_count]


def last_token(query_row, tail_rows, w_key, w_value, heads_count):
    tensor_count = lax.axis_size("tensor")
    col_count = tail_rows.shape[-1]
    tail = tail_rows.reshape(-1, col_count)
    features = w_key.shape[0]
    head_size = query_row.shape[0] // heads_count
    exact = lax.Precision.HIGHEST
    spread_query = jnp.einsum(
        "fhd,hd->hf",
        w_key.reshape(features, heads_count, head_size),
        query_row.reshape(heads_count, head_size),
        preferred_element_type=jnp.float32,
    )
    own_query = lax.all_to_all(
        spread_query.reshape(heads_count, tensor_count, col_count),
        "tensor",
        split_axis=1,
        concat_axis=0,
        tiled=True,
    ).reshape(-1, col_count)
    partial_scores = jnp.einsum(
        "hf,kf->hk", own_query, tail, precision=exact, preferred_element_type=jnp.float32
    )
    all_scores = lax.all_to_all(
        jnp.broadcast_to(partial_scores[None], (tensor_count,) + partial_scores.shape),
        "tensor",
        split_axis=0,
        concat_axis=0,
        tiled=True,
    )
    scores = jnp.sum(all_scores, axis=0) / jnp.sqrt(jnp.float32(head_size))
    top_score = jnp.max(scores, axis=-1, keepdims=True)
    weights_raw = jnp.exp(scores - top_score)
    soft = (weights_raw / jnp.sum(weights_raw, axis=-1, keepdims=True)).astype(jnp.bfloat16)
    mixed_rows = jnp.einsum("hk,kf->hf", soft, tail, preferred_element_type=jnp.float32)
    own_rows = lax.all_to_all(
        mixed_rows.reshape(tensor_count, heads_count, col_count),
        "tensor",
        split_axis=0,
        concat_axis=0,
        tiled=True,
    )
    own_rows = jnp.transpose(own_rows, (1, 0, 2)).reshape(heads_count, features)
    context = jnp.einsum(
        "hf,fhd->hd",
        own_rows,
        w_value.reshape(features, heads_count, head_size),
        precision=exact,
        preferred_element_type=jnp.float32,
    )
    return context.astype(jnp.bfloat16).reshape(-1)


def project_kernel(parts_ref, weight_ref, out_ref):
    total = jnp.dot(parts_ref[0, 0], weight_ref[0], preferred_element_type=jnp.float32)
    for part in range(1, parts_ref.shape[0]):
        total += jnp.dot(parts_ref[part, 0], weight_ref[part], preferred_element_type=jnp.float32)
    out_ref[0] = total.astype(out_ref.dtype)


def project(parts, weight):
    part_count, rows, ret_len, col_count = parts.shape
    out_cols = weight.shape[2]
    return pl.pallas_call(
        project_kernel,
        out_shape=jax.ShapeDtypeStruct((rows, ret_len, out_cols), jnp.bfloat16),
        grid=(rows,),
        in_specs=[
            pl.BlockSpec((part_count, 1, ret_len, col_count), lambda n: (0, n, 0, 0)),
            pl.BlockSpec(memory_space=pltpu.VMEM),
        ],
        out_specs=pl.BlockSpec((1, ret_len, out_cols), lambda n: (n, 0, 0)),
    )(parts, weight)


def shards(hidden, neighbour_ids, database, w_query, w_key, w_value, w_out):
    dp_count = lax.axis_size("dp")
    tok_rows = hidden.shape[0]
    group_count = neighbour_ids.shape[0]
    per_reader = group_count * neighbour_ids.shape[1]
    capacity = per_reader // 2
    db_count = database.shape[0]
    ret_len = database.shape[1]
    col_count = database.shape[2]
    head_cols = w_query.shape[1]
    heads_local = head_cols // HD
    tensor_count = lax.axis_size("tensor")
    group_len = tok_rows // group_count
    hidden_parts = lax.all_gather(hidden[group_len - 1 :], "tensor", axis=0, tiled=False)
    query_sum = jnp.einsum(
        "srf,sfc->rc",
        hidden_parts,
        w_query.reshape(tensor_count, -1, head_cols),
        preferred_element_type=jnp.float32,
    )
    query_rows = query_sum.astype(jnp.bfloat16)
    block_ids = neighbour_ids.reshape(per_reader)
    owners = block_ids // db_count
    earlier = jnp.arange(per_reader)[:, None] > jnp.arange(per_reader)[None, :]
    slot_rank = jnp.sum(((owners[:, None] == owners[None, :]) & earlier).astype(jnp.int32), 1)
    slot_range = jnp.arange(capacity, dtype=jnp.int32)
    local_index = block_ids % db_count
    owner_range = jnp.arange(dp_count, dtype=jnp.int32)
    slot_hit = (owners[:, None, None] == owner_range[None, :, None]) & (
        slot_rank[:, None, None] == slot_range[None, None, :]
    )
    request_table = jnp.sum(slot_hit.astype(jnp.int32) * local_index[:, None, None], 0)
    requested = lax.all_to_all(request_table, "dp", split_axis=0, concat_axis=0, tiled=True)
    outgoing = jnp.take(database, requested.reshape(-1), axis=0, mode="clip").reshape(
        dp_count, capacity, ret_len, col_count
    )
    arrived = lax.all_to_all(outgoing, "dp", split_axis=0, concat_axis=0, tiled=True)
    arrived_rows = arrived.reshape(dp_count * capacity, ret_len, col_count)
    arrived_slot = owners * capacity + slot_rank
    main_rows = per_reader - 2
    head_rows = jnp.take(arrived_rows, arrived_slot[:main_rows], axis=0, mode="clip")
    tail_rows = jnp.take(arrived_rows, arrived_slot[main_rows:], axis=0, mode="clip")
    main_parts = lax.all_gather(head_rows, "tensor", axis=0, tiled=False)
    w_key_parts = w_key.reshape(tensor_count, col_count, head_cols)
    w_value_parts = w_value.reshape(tensor_count, col_count, head_cols)
    w_both = lax.optimization_barrier(jnp.concatenate([w_key_parts, w_value_parts], axis=2))
    both_rows = project(main_parts, w_both)
    key_rows = both_rows[..., :head_cols].reshape(main_rows * ret_len, head_cols)
    value_rows = both_rows[..., head_cols:].reshape(main_rows * ret_len, head_cols)
    main_groups = main_rows // 2
    main_live = attend(
        query_rows[: main_groups * group_len], key_rows, value_rows, heads_local, group_len, main_groups
    )
    last_live = last_token(
        query_rows[main_groups * group_len], tail_rows, w_key, w_value, heads_local
    )
    live = jnp.concatenate([main_live, last_live[None]], 0)
    live_rows = live.shape[0]
    partial_out = jnp.einsum(
        "rc,csf->srf",
        live,
        w_out.reshape(head_cols, tensor_count, -1),
        preferred_element_type=jnp.float32,
    ).astype(jnp.bfloat16)
    spread = lax.all_to_all(partial_out, "tensor", split_axis=0, concat_axis=0, tiled=True)
    summed = jnp.sum(spread.astype(jnp.float32), axis=0).astype(jnp.bfloat16)
    return jnp.concatenate([jnp.zeros((group_len - 1, summed.shape[1]), jnp.bfloat16), summed], 0)


def solution(mesh):
    placed = (
        P("dp", "tensor"),
        P("dp", None),
        P("dp", None, "tensor"),
        P(None, "tensor"),
        P(None, "tensor"),
        P(None, "tensor"),
        P("tensor", None),
    )
    return jax.shard_map(
        shards, mesh=mesh, in_specs=placed, out_specs=P("dp", "tensor"), check_vma=False
    )
```

```python
import jax
import jax.numpy as jnp
from jax import lax
from jax.sharding import PartitionSpec as P

HD = 128


def attend(query_live, key_rows, value_rows, heads_count, group_len, groups):
    live_count, width = query_live.shape
    head_size = width // heads_count
    shifted = jnp.concatenate(
        [query_live, jnp.zeros((groups * group_len - live_count, width), jnp.bfloat16)], 0
    )
    shifted = shifted.reshape(groups, group_len, heads_count, head_size)
    key_block = key_rows.reshape(groups, -1, heads_count, head_size)
    value_block = value_rows.reshape(groups, -1, heads_count, head_size)
    scores = jnp.einsum(
        "cqhd,ckhd->chqk", shifted, key_block, preferred_element_type=jnp.float32
    ) / jnp.sqrt(jnp.float32(head_size))
    top_score = jnp.max(scores, axis=-1, keepdims=True)
    weights_raw = jnp.exp(scores - top_score)
    soft = (weights_raw / jnp.sum(weights_raw, axis=-1, keepdims=True)).astype(jnp.bfloat16)
    blended = jnp.einsum(
        "chqk,ckhd->cqhd", soft, value_block, preferred_element_type=jnp.float32
    ).astype(jnp.bfloat16)
    return blended.reshape(groups * group_len, width)[:live_count]


def last_token(query_row, tail_rows, w_key, w_value, heads_count):
    tensor_count = lax.axis_size("tensor")
    col_count = tail_rows.shape[-1]
    tail = tail_rows.reshape(-1, col_count)
    features = w_key.shape[0]
    head_size = query_row.shape[0] // heads_count
    exact = lax.Precision.HIGHEST
    spread_query = jnp.einsum(
        "fhd,hd->hf",
        w_key.reshape(features, heads_count, head_size),
        query_row.reshape(heads_count, head_size),
        preferred_element_type=jnp.float32,
    )
    own_query = lax.all_to_all(
        spread_query.reshape(heads_count, tensor_count, col_count),
        "tensor",
        split_axis=1,
        concat_axis=0,
        tiled=True,
    ).reshape(-1, col_count)
    partial_scores = jnp.einsum(
        "hf,kf->hk", own_query, tail, precision=exact, preferred_element_type=jnp.float32
    )
    all_scores = lax.all_to_all(
        jnp.broadcast_to(partial_scores[None], (tensor_count,) + partial_scores.shape),
        "tensor",
        split_axis=0,
        concat_axis=0,
        tiled=True,
    )
    scores = jnp.sum(all_scores, axis=0) / jnp.sqrt(jnp.float32(head_size))
    top_score = jnp.max(scores, axis=-1, keepdims=True)
    weights_raw = jnp.exp(scores - top_score)
    soft = (weights_raw / jnp.sum(weights_raw, axis=-1, keepdims=True)).astype(jnp.bfloat16)
    mixed_rows = jnp.einsum("hk,kf->hf", soft, tail, preferred_element_type=jnp.float32)
    own_rows = lax.all_to_all(
        mixed_rows.reshape(tensor_count, heads_count, col_count),
        "tensor",
        split_axis=0,
        concat_axis=0,
        tiled=True,
    )
    own_rows = jnp.transpose(own_rows, (1, 0, 2)).reshape(heads_count, features)
    context = jnp.einsum(
        "hf,fhd->hd",
        own_rows,
        w_value.reshape(features, heads_count, head_size),
        precision=exact,
        preferred_element_type=jnp.float32,
    )
    return context.astype(jnp.bfloat16).reshape(-1)


def shards(hidden, neighbour_ids, database, w_query, w_key, w_value, w_out):
    dp_count = lax.axis_size("dp")
    tok_rows = hidden.shape[0]
    group_count = neighbour_ids.shape[0]
    per_reader = group_count * neighbour_ids.shape[1]
    capacity = per_reader // 2
    db_count = database.shape[0]
    ret_len = database.shape[1]
    col_count = database.shape[2]
    head_cols = w_query.shape[1]
    heads_local = head_cols // HD
    tensor_count = lax.axis_size("tensor")
    group_len = tok_rows // group_count
    hidden_parts = lax.all_gather(hidden, "tensor", axis=0, tiled=False)
    query_sum = jnp.einsum(
        "srf,sfc->rc",
        hidden_parts[:, group_len - 1 :],
        w_query.reshape(tensor_count, -1, head_cols),
        preferred_element_type=jnp.float32,
    )
    query_rows = query_sum.astype(jnp.bfloat16)
    block_ids = neighbour_ids.reshape(per_reader)
    owners = block_ids // db_count
    earlier = jnp.arange(per_reader)[:, None] > jnp.arange(per_reader)[None, :]
    slot_rank = jnp.sum(((owners[:, None] == owners[None, :]) & earlier).astype(jnp.int32), 1)
    slot_range = jnp.arange(capacity, dtype=jnp.int32)
    local_index = block_ids % db_count
    owner_range = jnp.arange(dp_count, dtype=jnp.int32)
    slot_hit = (owners[:, None, None] == owner_range[None, :, None]) & (
        slot_rank[:, None, None] == slot_range[None, None, :]
    )
    request_table = jnp.sum(slot_hit.astype(jnp.int32) * local_index[:, None, None], 0)
    requested = lax.all_to_all(request_table, "dp", split_axis=0, concat_axis=0, tiled=True)
    outgoing = jnp.take(database, requested.reshape(-1), axis=0, mode="clip").reshape(
        dp_count, capacity, ret_len, col_count
    )
    arrived = lax.all_to_all(outgoing, "dp", split_axis=0, concat_axis=0, tiled=True)
    arrived_rows = arrived.reshape(dp_count * capacity, ret_len, col_count)
    arrived_slot = owners * capacity + slot_rank
    main_rows = per_reader - 2
    head_rows = jnp.take(arrived_rows, arrived_slot[:main_rows], axis=0, mode="clip")
    tail_rows = jnp.take(arrived_rows, arrived_slot[main_rows:], axis=0, mode="clip")
    main_parts = lax.all_gather(head_rows, "tensor", axis=0, tiled=False)
    w_key_parts = w_key.reshape(tensor_count, col_count, head_cols)
    w_value_parts = w_value.reshape(tensor_count, col_count, head_cols)
    w_both = lax.optimization_barrier(jnp.concatenate([w_key_parts, w_value_parts], axis=2))
    both_rows = jnp.einsum(
        "snkf,sfc->nkc", main_parts, w_both, preferred_element_type=jnp.float32
    ).astype(jnp.bfloat16)
    key_rows = both_rows[..., :head_cols].reshape(main_rows * ret_len, head_cols)
    value_rows = both_rows[..., head_cols:].reshape(main_rows * ret_len, head_cols)
    main_groups = main_rows // 2
    main_live = attend(
        query_rows[: main_groups * group_len], key_rows, value_rows, heads_local, group_len, main_groups
    )
    last_live = last_token(
        query_rows[main_groups * group_len], tail_rows, w_key, w_value, heads_local
    )
    live = jnp.concatenate([main_live, last_live[None]], 0)
    live_rows = live.shape[0]
    partial_out = jnp.einsum(
        "rc,csf->srf",
        live,
        w_out.reshape(head_cols, tensor_count, -1),
        preferred_element_type=jnp.float32,
    ).astype(jnp.bfloat16)
    spread = lax.all_to_all(partial_out, "tensor", split_axis=0, concat_axis=0, tiled=True)
    summed = jnp.sum(spread.astype(jnp.float32), axis=0).astype(jnp.bfloat16)
    return jnp.concatenate([jnp.zeros((group_len - 1, summed.shape[1]), jnp.bfloat16), summed], 0)


def solution(mesh):
    placed = (
        P("dp", "tensor"),
        P("dp", None),
        P("dp", None, "tensor"),
        P(None, "tensor"),
        P(None, "tensor"),
        P(None, "tensor"),
        P("tensor", None),
    )
    return jax.shard_map(
        shards, mesh=mesh, in_specs=placed, out_specs=P("dp", "tensor"), check_vma=False
    )
```

```python
import jax
import jax.numpy as jnp
from jax import lax
from jax.sharding import PartitionSpec as P

HD = 128


def attend(query_live, key_rows, value_rows, heads_count, group_len, groups):
    live_count, width = query_live.shape
    head_size = width // heads_count
    shifted = jnp.concatenate(
        [query_live, jnp.zeros((groups * group_len - live_count, width), jnp.bfloat16)], 0
    )
    shifted = shifted.reshape(groups, group_len, heads_count, head_size)
    key_block = key_rows.reshape(groups, -1, heads_count, head_size)
    value_block = value_rows.reshape(groups, -1, heads_count, head_size)
    scores = jnp.einsum(
        "cqhd,ckhd->chqk", shifted, key_block, preferred_element_type=jnp.float32
    ) / jnp.sqrt(jnp.float32(head_size))
    top_score = jnp.max(scores, axis=-1, keepdims=True)
    weights_raw = jnp.exp(scores - top_score)
    soft = (weights_raw / jnp.sum(weights_raw, axis=-1, keepdims=True)).astype(jnp.bfloat16)
    blended = jnp.einsum(
        "chqk,ckhd->cqhd", soft, value_block, preferred_element_type=jnp.float32
    ).astype(jnp.bfloat16)
    return blended.reshape(groups * group_len, width)[:live_count]


def last_token(query_row, tail_rows, w_key, w_value, heads_count):
    tensor_count = lax.axis_size("tensor")
    col_count = tail_rows.shape[-1]
    tail = tail_rows.reshape(-1, col_count)
    features = w_key.shape[0]
    head_size = query_row.shape[0] // heads_count
    exact = lax.Precision.HIGHEST
    spread_query = jnp.einsum(
        "fhd,hd->hf",
        w_key.reshape(features, heads_count, head_size),
        query_row.reshape(heads_count, head_size),
        preferred_element_type=jnp.float32,
    )
    own_query = lax.all_to_all(
        spread_query.reshape(heads_count, tensor_count, col_count),
        "tensor",
        split_axis=1,
        concat_axis=0,
        tiled=True,
    ).reshape(-1, col_count)
    partial_scores = jnp.einsum(
        "hf,kf->hk", own_query, tail, precision=exact, preferred_element_type=jnp.float32
    )
    all_scores = lax.all_to_all(
        jnp.broadcast_to(partial_scores[None], (tensor_count,) + partial_scores.shape),
        "tensor",
        split_axis=0,
        concat_axis=0,
        tiled=True,
    )
    scores = jnp.sum(all_scores, axis=0) / jnp.sqrt(jnp.float32(head_size))
    top_score = jnp.max(scores, axis=-1, keepdims=True)
    weights_raw = jnp.exp(scores - top_score)
    soft = (weights_raw / jnp.sum(weights_raw, axis=-1, keepdims=True)).astype(jnp.bfloat16)
    mixed_rows = jnp.einsum("hk,kf->hf", soft, tail, preferred_element_type=jnp.float32)
    own_rows = lax.all_to_all(
        mixed_rows.reshape(tensor_count, heads_count, col_count),
        "tensor",
        split_axis=0,
        concat_axis=0,
        tiled=True,
    )
    own_rows = jnp.transpose(own_rows, (1, 0, 2)).reshape(heads_count, features)
    context = jnp.einsum(
        "hf,fhd->hd",
        own_rows,
        w_value.reshape(features, heads_count, head_size),
        precision=exact,
        preferred_element_type=jnp.float32,
    )
    return context.astype(jnp.bfloat16).reshape(-1)


def shards(hidden, neighbour_ids, database, w_query, w_key, w_value, w_out):
    dp_count = lax.axis_size("dp")
    tok_rows = hidden.shape[0]
    group_count = neighbour_ids.shape[0]
    per_reader = group_count * neighbour_ids.shape[1]
    capacity = per_reader // 2
    db_count = database.shape[0]
    ret_len = database.shape[1]
    col_count = database.shape[2]
    head_cols = w_query.shape[1]
    heads_local = head_cols // HD
    tensor_count = lax.axis_size("tensor")
    group_len = tok_rows // group_count
    hidden_parts = lax.all_gather(hidden, "tensor", axis=0, tiled=False)
    query_sum = jnp.einsum(
        "srf,sfc->rc",
        hidden_parts[:, group_len - 1 :],
        w_query.reshape(tensor_count, -1, head_cols),
        preferred_element_type=jnp.float32,
    )
    query_rows = query_sum.astype(jnp.bfloat16)
    block_ids = neighbour_ids.reshape(per_reader)
    owners = block_ids // db_count
    earlier = jnp.arange(per_reader)[:, None] > jnp.arange(per_reader)[None, :]
    slot_rank = jnp.sum(((owners[:, None] == owners[None, :]) & earlier).astype(jnp.int32), 1)
    slot_range = jnp.arange(capacity, dtype=jnp.int32)
    local_index = block_ids % db_count
    owner_range = jnp.arange(dp_count, dtype=jnp.int32)
    slot_hit = (owners[:, None, None] == owner_range[None, :, None]) & (
        slot_rank[:, None, None] == slot_range[None, None, :]
    )
    request_table = jnp.sum(slot_hit.astype(jnp.int32) * local_index[:, None, None], 0)
    requested = lax.all_to_all(request_table, "dp", split_axis=0, concat_axis=0, tiled=True)
    outgoing = jnp.take(database, requested.reshape(-1), axis=0, mode="clip").reshape(
        dp_count, capacity, ret_len, col_count
    )
    arrived = lax.all_to_all(outgoing, "dp", split_axis=0, concat_axis=0, tiled=True)
    arrived_rows = arrived.reshape(dp_count * capacity, ret_len, col_count)
    arrived_slot = owners * capacity + slot_rank
    main_rows = per_reader - 2
    head_rows = jnp.take(arrived_rows, arrived_slot[:main_rows], axis=0, mode="clip")
    tail_rows = jnp.take(arrived_rows, arrived_slot[main_rows:], axis=0, mode="clip")
    main_parts = lax.all_gather(head_rows, "tensor", axis=0, tiled=False)
    w_key_parts = w_key.reshape(tensor_count, col_count, head_cols)
    w_value_parts = w_value.reshape(tensor_count, col_count, head_cols)
    w_both = lax.optimization_barrier(jnp.concatenate([w_key_parts, w_value_parts], axis=2))
    both_rows = jnp.einsum(
        "snkf,sfc->nkc", main_parts, w_both, preferred_element_type=jnp.float32
    ).astype(jnp.bfloat16)
    key_rows = both_rows[..., :head_cols].reshape(main_rows * ret_len, head_cols)
    value_rows = both_rows[..., head_cols:].reshape(main_rows * ret_len, head_cols)
    main_groups = main_rows // 2
    main_live = attend(
        query_rows[: main_groups * group_len], key_rows, value_rows, heads_local, group_len, main_groups
    )
    last_live = last_token(
        query_rows[main_groups * group_len], tail_rows, w_key, w_value, heads_local
    )
    w_out_parts = w_out.reshape(head_cols, tensor_count, -1)
    last_partial = jnp.einsum(
        "c,csf->sf", last_live, w_out_parts, preferred_element_type=jnp.float32
    ).astype(jnp.bfloat16)
    last_spread = lax.all_to_all(last_partial, "tensor", split_axis=0, concat_axis=0, tiled=True)
    last_sum = jnp.sum(last_spread.astype(jnp.float32), axis=0).astype(jnp.bfloat16)
    partial_out = jnp.einsum(
        "rc,csf->srf", main_live, w_out_parts, preferred_element_type=jnp.float32
    ).astype(jnp.bfloat16)
    spread = lax.all_to_all(partial_out, "tensor", split_axis=0, concat_axis=0, tiled=True)
    summed = jnp.concatenate(
        [jnp.sum(spread.astype(jnp.float32), axis=0).astype(jnp.bfloat16), last_sum[None]], 0
    )
    return jnp.concatenate([jnp.zeros((group_len - 1, summed.shape[1]), jnp.bfloat16), summed], 0)


def solution(mesh):
    placed = (
        P("dp", "tensor"),
        P("dp", None),
        P("dp", None, "tensor"),
        P(None, "tensor"),
        P(None, "tensor"),
        P(None, "tensor"),
        P("tensor", None),
    )
    return jax.shard_map(
        shards, mesh=mesh, in_specs=placed, out_specs=P("dp", "tensor"), check_vma=False
    )
```

```python
import jax
import jax.numpy as jnp
from jax import lax
from jax.sharding import PartitionSpec as P
from jax.experimental import pallas as pl
from jax.experimental.pallas import tpu as pltpu

HD = 128


def attend(query_live, key_rows, value_rows, heads_count, group_len, groups):
    live_count, width = query_live.shape
    head_size = width // heads_count
    shifted = jnp.concatenate(
        [query_live, jnp.zeros((groups * group_len - live_count, width), jnp.bfloat16)], 0
    )
    shifted = shifted.reshape(groups, group_len, heads_count, head_size)
    key_block = key_rows.reshape(groups, -1, heads_count, head_size)
    value_block = value_rows.reshape(groups, -1, heads_count, head_size)
    scores = jnp.einsum(
        "cqhd,ckhd->chqk", shifted, key_block, preferred_element_type=jnp.float32
    ) / jnp.sqrt(jnp.float32(head_size))
    top_score = jnp.max(scores, axis=-1, keepdims=True)
    weights_raw = jnp.exp(scores - top_score)
    soft = (weights_raw / jnp.sum(weights_raw, axis=-1, keepdims=True)).astype(jnp.bfloat16)
    blended = jnp.einsum(
        "chqk,ckhd->cqhd", soft, value_block, preferred_element_type=jnp.float32
    ).astype(jnp.bfloat16)
    return blended.reshape(groups * group_len, width)[:live_count]


def last_token(query_row, tail_rows, w_key, w_value, heads_count):
    tensor_count = lax.axis_size("tensor")
    col_count = tail_rows.shape[-1]
    tail = tail_rows.reshape(-1, col_count)
    features = w_key.shape[0]
    head_size = query_row.shape[0] // heads_count
    exact = lax.Precision.HIGHEST
    spread_query = jnp.einsum(
        "fhd,hd->hf",
        w_key.reshape(features, heads_count, head_size),
        query_row.reshape(heads_count, head_size),
        preferred_element_type=jnp.float32,
    )
    own_query = lax.all_to_all(
        spread_query.reshape(heads_count, tensor_count, col_count),
        "tensor",
        split_axis=1,
        concat_axis=0,
        tiled=True,
    ).reshape(-1, col_count)
    partial_scores = jnp.einsum(
        "hf,kf->hk", own_query, tail, precision=exact, preferred_element_type=jnp.float32
    )
    all_scores = lax.all_to_all(
        jnp.broadcast_to(partial_scores[None], (tensor_count,) + partial_scores.shape),
        "tensor",
        split_axis=0,
        concat_axis=0,
        tiled=True,
    )
    scores = jnp.sum(all_scores, axis=0) / jnp.sqrt(jnp.float32(head_size))
    top_score = jnp.max(scores, axis=-1, keepdims=True)
    weights_raw = jnp.exp(scores - top_score)
    soft = (weights_raw / jnp.sum(weights_raw, axis=-1, keepdims=True)).astype(jnp.bfloat16)
    mixed_rows = jnp.einsum("hk,kf->hf", soft, tail, preferred_element_type=jnp.float32)
    own_rows = lax.all_to_all(
        mixed_rows.reshape(tensor_count, heads_count, col_count),
        "tensor",
        split_axis=0,
        concat_axis=0,
        tiled=True,
    )
    own_rows = jnp.transpose(own_rows, (1, 0, 2)).reshape(heads_count, features)
    context = jnp.einsum(
        "hf,fhd->hd",
        own_rows,
        w_value.reshape(features, heads_count, head_size),
        precision=exact,
        preferred_element_type=jnp.float32,
    )
    return context.astype(jnp.bfloat16).reshape(-1)


def pick_kernel(index_ref, source_ref, out_ref, sems):
    last = source_ref.shape[0] - 1
    copies = []
    for n in range(out_ref.shape[0]):
        row = jnp.minimum(jnp.maximum(index_ref[n], 0), last)
        copies.append(pltpu.make_async_copy(source_ref.at[row], out_ref.at[n], sems.at[n]))
    for copy in copies:
        copy.start()
    for copy in copies:
        copy.wait()


def pick(source, index):
    count = index.shape[0]
    return pl.pallas_call(
        pick_kernel,
        out_shape=jax.ShapeDtypeStruct((count,) + source.shape[1:], source.dtype),
        in_specs=[pl.BlockSpec(memory_space=pltpu.SMEM), pl.BlockSpec(memory_space=pl.ANY)],
        out_specs=pl.BlockSpec(memory_space=pl.ANY),
        scratch_shapes=[pltpu.SemaphoreType.DMA((count,))],
    )(index, source)


def shards(hidden, neighbour_ids, database, w_query, w_key, w_value, w_out):
    dp_count = lax.axis_size("dp")
    tok_rows = hidden.shape[0]
    group_count = neighbour_ids.shape[0]
    per_reader = group_count * neighbour_ids.shape[1]
    capacity = per_reader // 2
    db_count = database.shape[0]
    ret_len = database.shape[1]
    col_count = database.shape[2]
    head_cols = w_query.shape[1]
    heads_local = head_cols // HD
    tensor_count = lax.axis_size("tensor")
    group_len = tok_rows // group_count
    hidden_parts = lax.all_gather(hidden, "tensor", axis=0, tiled=False)
    query_sum = jnp.einsum(
        "srf,sfc->rc",
        hidden_parts[:, group_len - 1 :],
        w_query.reshape(tensor_count, -1, head_cols),
        preferred_element_type=jnp.float32,
    )
    query_rows = query_sum.astype(jnp.bfloat16)
    block_ids = neighbour_ids.reshape(per_reader)
    owners = block_ids // db_count
    earlier = jnp.arange(per_reader)[:, None] > jnp.arange(per_reader)[None, :]
    slot_rank = jnp.sum(((owners[:, None] == owners[None, :]) & earlier).astype(jnp.int32), 1)
    slot_range = jnp.arange(capacity, dtype=jnp.int32)
    local_index = block_ids % db_count
    owner_range = jnp.arange(dp_count, dtype=jnp.int32)
    slot_hit = (owners[:, None, None] == owner_range[None, :, None]) & (
        slot_rank[:, None, None] == slot_range[None, None, :]
    )
    request_table = jnp.sum(slot_hit.astype(jnp.int32) * local_index[:, None, None], 0)
    requested = lax.all_to_all(request_table, "dp", split_axis=0, concat_axis=0, tiled=True)
    outgoing = pick(database, requested.reshape(-1)).reshape(
        dp_count, capacity, ret_len, col_count
    )
    arrived = lax.all_to_all(outgoing, "dp", split_axis=0, concat_axis=0, tiled=True)
    arrived_rows = arrived.reshape(dp_count * capacity, ret_len, col_count)
    arrived_slot = owners * capacity + slot_rank
    main_rows = per_reader - 2
    head_rows = pick(arrived_rows, arrived_slot[:main_rows])
    tail_rows = jnp.take(arrived_rows, arrived_slot[main_rows:], axis=0, mode="clip")
    main_parts = lax.all_gather(head_rows, "tensor", axis=0, tiled=False)
    w_key_parts = w_key.reshape(tensor_count, col_count, head_cols)
    w_value_parts = w_value.reshape(tensor_count, col_count, head_cols)
    w_both = lax.optimization_barrier(jnp.concatenate([w_key_parts, w_value_parts], axis=2))
    both_rows = jnp.einsum(
        "snkf,sfc->nkc", main_parts, w_both, preferred_element_type=jnp.float32
    ).astype(jnp.bfloat16)
    key_rows = both_rows[..., :head_cols].reshape(main_rows * ret_len, head_cols)
    value_rows = both_rows[..., head_cols:].reshape(main_rows * ret_len, head_cols)
    main_groups = main_rows // 2
    main_live = attend(
        query_rows[: main_groups * group_len], key_rows, value_rows, heads_local, group_len, main_groups
    )
    last_live = last_token(
        query_rows[main_groups * group_len], tail_rows, w_key, w_value, heads_local
    )
    live = jnp.concatenate([main_live, last_live[None]], 0)
    live_rows = live.shape[0]
    partial_out = jnp.einsum(
        "rc,csf->srf",
        live,
        w_out.reshape(head_cols, tensor_count, -1),
        preferred_element_type=jnp.float32,
    ).astype(jnp.bfloat16)
    spread = lax.all_to_all(partial_out, "tensor", split_axis=0, concat_axis=0, tiled=True)
    summed = jnp.sum(spread.astype(jnp.float32), axis=0).astype(jnp.bfloat16)
    return jnp.concatenate([jnp.zeros((group_len - 1, summed.shape[1]), jnp.bfloat16), summed], 0)


def solution(mesh):
    placed = (
        P("dp", "tensor"),
        P("dp", None),
        P("dp", None, "tensor"),
        P(None, "tensor"),
        P(None, "tensor"),
        P(None, "tensor"),
        P("tensor", None),
    )
    return jax.shard_map(
        shards, mesh=mesh, in_specs=placed, out_specs=P("dp", "tensor"), check_vma=False
    )
```

```python
import jax
import jax.numpy as jnp
from jax import lax
from jax.sharding import PartitionSpec as P

HD = 128


def attend(query_live, key_rows, value_rows, heads_count, group_len, groups):
    live_count, width = query_live.shape
    head_size = width // heads_count
    shifted = jnp.concatenate(
        [query_live, jnp.zeros((groups * group_len - live_count, width), jnp.bfloat16)], 0
    )
    shifted = shifted.reshape(groups, group_len, heads_count, head_size)
    key_block = key_rows.reshape(groups, -1, heads_count, head_size)
    value_block = value_rows.reshape(groups, -1, heads_count, head_size)
    scores = jnp.einsum(
        "cqhd,ckhd->chqk", shifted, key_block, preferred_element_type=jnp.float32
    ) / jnp.sqrt(jnp.float32(head_size))
    top_score = jnp.max(scores, axis=-1, keepdims=True)
    weights_raw = jnp.exp(scores - top_score)
    soft = (weights_raw / jnp.sum(weights_raw, axis=-1, keepdims=True)).astype(jnp.bfloat16)
    blended = jnp.einsum(
        "chqk,ckhd->cqhd", soft, value_block, preferred_element_type=jnp.float32
    ).astype(jnp.bfloat16)
    return blended.reshape(groups * group_len, width)[:live_count]


def last_token(query_row, tail_rows, w_key, w_value, heads_count):
    tensor_count = lax.axis_size("tensor")
    col_count = tail_rows.shape[-1]
    tail = tail_rows.reshape(-1, col_count)
    features = w_key.shape[0]
    head_size = query_row.shape[0] // heads_count
    exact = lax.Precision.HIGHEST
    spread_query = jnp.einsum(
        "fhd,hd->hf",
        w_key.reshape(features, heads_count, head_size),
        query_row.reshape(heads_count, head_size),
        preferred_element_type=jnp.float32,
    )
    own_query = lax.all_to_all(
        spread_query.reshape(heads_count, tensor_count, col_count),
        "tensor",
        split_axis=1,
        concat_axis=0,
        tiled=True,
    ).reshape(-1, col_count)
    partial_scores = jnp.einsum(
        "hf,kf->hk", own_query, tail, precision=exact, preferred_element_type=jnp.float32
    )
    own_scores = lax.all_to_all(
        partial_scores.reshape(tensor_count, heads_count, -1),
        "tensor",
        split_axis=0,
        concat_axis=0,
        tiled=True,
    )
    scores = jnp.sum(own_scores, axis=0) / jnp.sqrt(jnp.float32(head_size))
    top_score = jnp.max(scores, axis=-1, keepdims=True)
    weights_raw = jnp.exp(scores - top_score)
    own_soft = (weights_raw / jnp.sum(weights_raw, axis=-1, keepdims=True)).astype(jnp.bfloat16)
    soft = lax.all_to_all(
        jnp.broadcast_to(own_soft[None], (tensor_count,) + own_soft.shape),
        "tensor",
        split_axis=0,
        concat_axis=0,
        tiled=True,
    ).reshape(tensor_count * heads_count, -1)
    mixed_rows = jnp.einsum("hk,kf->hf", soft, tail, preferred_element_type=jnp.float32)
    own_rows = lax.all_to_all(
        mixed_rows.reshape(tensor_count, heads_count, col_count),
        "tensor",
        split_axis=0,
        concat_axis=0,
        tiled=True,
    )
    own_rows = jnp.transpose(own_rows, (1, 0, 2)).reshape(heads_count, features)
    context = jnp.einsum(
        "hf,fhd->hd",
        own_rows,
        w_value.reshape(features, heads_count, head_size),
        precision=exact,
        preferred_element_type=jnp.float32,
    )
    return context.astype(jnp.bfloat16).reshape(-1)


def shards(hidden, neighbour_ids, database, w_query, w_key, w_value, w_out):
    dp_count = lax.axis_size("dp")
    tok_rows = hidden.shape[0]
    group_count = neighbour_ids.shape[0]
    per_reader = group_count * neighbour_ids.shape[1]
    capacity = per_reader // 2
    db_count = database.shape[0]
    ret_len = database.shape[1]
    col_count = database.shape[2]
    head_cols = w_query.shape[1]
    heads_local = head_cols // HD
    tensor_count = lax.axis_size("tensor")
    group_len = tok_rows // group_count
    hidden_parts = lax.all_gather(hidden, "tensor", axis=0, tiled=False)
    query_sum = jnp.einsum(
        "srf,sfc->rc",
        hidden_parts[:, group_len - 1 :],
        w_query.reshape(tensor_count, -1, head_cols),
        preferred_element_type=jnp.float32,
    )
    query_rows = query_sum.astype(jnp.bfloat16)
    block_ids = neighbour_ids.reshape(per_reader)
    owners = block_ids // db_count
    earlier = jnp.arange(per_reader)[:, None] > jnp.arange(per_reader)[None, :]
    slot_rank = jnp.sum(((owners[:, None] == owners[None, :]) & earlier).astype(jnp.int32), 1)
    slot_range = jnp.arange(capacity, dtype=jnp.int32)
    local_index = block_ids % db_count
    owner_range = jnp.arange(dp_count, dtype=jnp.int32)
    slot_hit = (owners[:, None, None] == owner_range[None, :, None]) & (
        slot_rank[:, None, None] == slot_range[None, None, :]
    )
    request_table = jnp.sum(slot_hit.astype(jnp.int32) * local_index[:, None, None], 0)
    requested = lax.all_to_all(request_table, "dp", split_axis=0, concat_axis=0, tiled=True)
    outgoing = jnp.take(database, requested.reshape(-1), axis=0, mode="clip").reshape(
        dp_count, capacity, ret_len, col_count
    )
    arrived = lax.all_to_all(outgoing, "dp", split_axis=0, concat_axis=0, tiled=True)
    arrived_rows = arrived.reshape(dp_count * capacity, ret_len, col_count)
    arrived_slot = owners * capacity + slot_rank
    main_rows = per_reader - 2
    head_rows = jnp.take(arrived_rows, arrived_slot[:main_rows], axis=0, mode="clip")
    tail_rows = jnp.take(arrived_rows, arrived_slot[main_rows:], axis=0, mode="clip")
    main_parts = lax.all_gather(head_rows, "tensor", axis=0, tiled=False)
    w_key_parts = w_key.reshape(tensor_count, col_count, head_cols)
    w_value_parts = w_value.reshape(tensor_count, col_count, head_cols)
    w_both = lax.optimization_barrier(jnp.concatenate([w_key_parts, w_value_parts], axis=2))
    both_rows = jnp.einsum(
        "snkf,sfc->nkc", main_parts, w_both, preferred_element_type=jnp.float32
    ).astype(jnp.bfloat16)
    key_rows = both_rows[..., :head_cols].reshape(main_rows * ret_len, head_cols)
    value_rows = both_rows[..., head_cols:].reshape(main_rows * ret_len, head_cols)
    main_groups = main_rows // 2
    main_live = attend(
        query_rows[: main_groups * group_len], key_rows, value_rows, heads_local, group_len, main_groups
    )
    last_live = last_token(
        query_rows[main_groups * group_len], tail_rows, w_key, w_value, heads_local
    )
    live = jnp.concatenate([main_live, last_live[None]], 0)
    live_rows = live.shape[0]
    partial_out = jnp.einsum(
        "rc,csf->srf",
        live,
        w_out.reshape(head_cols, tensor_count, -1),
        preferred_element_type=jnp.float32,
    ).astype(jnp.bfloat16)
    spread = lax.all_to_all(partial_out, "tensor", split_axis=0, concat_axis=0, tiled=True)
    summed = jnp.sum(spread.astype(jnp.float32), axis=0).astype(jnp.bfloat16)
    return jnp.concatenate([jnp.zeros((group_len - 1, summed.shape[1]), jnp.bfloat16), summed], 0)


def solution(mesh):
    placed = (
        P("dp", "tensor"),
        P("dp", None),
        P("dp", None, "tensor"),
        P(None, "tensor"),
        P(None, "tensor"),
        P(None, "tensor"),
        P("tensor", None),
    )
    return jax.shard_map(
        shards, mesh=mesh, in_specs=placed, out_specs=P("dp", "tensor"), check_vma=False
    )
```

```python
import jax
import jax.numpy as jnp
from jax import lax
from jax.sharding import PartitionSpec as P
from jax.experimental import pallas as pl
from jax.experimental.pallas import tpu as pltpu

HD = 128


def attend(query_live, key_rows, value_rows, heads_count, group_len, groups):
    live_count, width = query_live.shape
    head_size = width // heads_count
    shifted = jnp.concatenate(
        [query_live, jnp.zeros((groups * group_len - live_count, width), jnp.bfloat16)], 0
    )
    shifted = shifted.reshape(groups, group_len, heads_count, head_size)
    key_block = key_rows.reshape(groups, -1, heads_count, head_size)
    value_block = value_rows.reshape(groups, -1, heads_count, head_size)
    scores = jnp.einsum(
        "cqhd,ckhd->chqk", shifted, key_block, preferred_element_type=jnp.float32
    ) / jnp.sqrt(jnp.float32(head_size))
    top_score = jnp.max(scores, axis=-1, keepdims=True)
    weights_raw = jnp.exp(scores - top_score)
    soft = (weights_raw / jnp.sum(weights_raw, axis=-1, keepdims=True)).astype(jnp.bfloat16)
    blended = jnp.einsum(
        "chqk,ckhd->cqhd", soft, value_block, preferred_element_type=jnp.float32
    ).astype(jnp.bfloat16)
    return blended.reshape(groups * group_len, width)[:live_count]


def last_token(query_row, tail_rows, w_key, w_value, heads_count):
    tensor_count = lax.axis_size("tensor")
    col_count = tail_rows.shape[-1]
    tail = tail_rows.reshape(-1, col_count)
    features = w_key.shape[0]
    head_size = query_row.shape[0] // heads_count
    exact = lax.Precision.HIGHEST
    spread_query = jnp.einsum(
        "fhd,hd->hf",
        w_key.reshape(features, heads_count, head_size),
        query_row.reshape(heads_count, head_size),
        preferred_element_type=jnp.float32,
    )
    own_query = lax.all_to_all(
        spread_query.reshape(heads_count, tensor_count, col_count),
        "tensor",
        split_axis=1,
        concat_axis=0,
        tiled=True,
    ).reshape(-1, col_count)
    partial_scores = jnp.einsum(
        "hf,kf->hk", own_query, tail, precision=exact, preferred_element_type=jnp.float32
    )
    all_scores = lax.all_to_all(
        jnp.broadcast_to(partial_scores[None], (tensor_count,) + partial_scores.shape),
        "tensor",
        split_axis=0,
        concat_axis=0,
        tiled=True,
    )
    scores = jnp.sum(all_scores, axis=0) / jnp.sqrt(jnp.float32(head_size))
    top_score = jnp.max(scores, axis=-1, keepdims=True)
    weights_raw = jnp.exp(scores - top_score)
    soft = (weights_raw / jnp.sum(weights_raw, axis=-1, keepdims=True)).astype(jnp.bfloat16)
    mixed_rows = jnp.einsum("hk,kf->hf", soft, tail, preferred_element_type=jnp.float32)
    own_rows = lax.all_to_all(
        mixed_rows.reshape(tensor_count, heads_count, col_count),
        "tensor",
        split_axis=0,
        concat_axis=0,
        tiled=True,
    )
    own_rows = jnp.transpose(own_rows, (1, 0, 2)).reshape(heads_count, features)
    context = jnp.einsum(
        "hf,fhd->hd",
        own_rows,
        w_value.reshape(features, heads_count, head_size),
        precision=exact,
        preferred_element_type=jnp.float32,
    )
    return context.astype(jnp.bfloat16).reshape(-1)


def copy_kernel(index_ref, source_ref, out_ref):
    out_ref[...] = source_ref[...]


def pick(source, index):
    count = index.shape[0]
    block = (1,) + source.shape[1:]
    tail = (0,) * (source.ndim - 1)
    return pl.pallas_call(
        copy_kernel,
        out_shape=jax.ShapeDtypeStruct((count,) + source.shape[1:], source.dtype),
        grid_spec=pltpu.PrefetchScalarGridSpec(
            num_scalar_prefetch=1,
            grid=(count,),
            in_specs=[pl.BlockSpec(block, lambda n, rows: (rows[n],) + tail)],
            out_specs=pl.BlockSpec(block, lambda n, rows: (n,) + tail),
        ),
    )(jnp.clip(index, 0, source.shape[0] - 1), source)


def shards(hidden, neighbour_ids, database, w_query, w_key, w_value, w_out):
    dp_count = lax.axis_size("dp")
    tok_rows = hidden.shape[0]
    group_count = neighbour_ids.shape[0]
    per_reader = group_count * neighbour_ids.shape[1]
    capacity = per_reader // 2
    db_count = database.shape[0]
    ret_len = database.shape[1]
    col_count = database.shape[2]
    head_cols = w_query.shape[1]
    heads_local = head_cols // HD
    tensor_count = lax.axis_size("tensor")
    group_len = tok_rows // group_count
    hidden_parts = lax.all_gather(hidden, "tensor", axis=0, tiled=False)
    query_sum = jnp.einsum(
        "srf,sfc->rc",
        hidden_parts[:, group_len - 1 :],
        w_query.reshape(tensor_count, -1, head_cols),
        preferred_element_type=jnp.float32,
    )
    query_rows = query_sum.astype(jnp.bfloat16)
    block_ids = neighbour_ids.reshape(per_reader)
    owners = block_ids // db_count
    earlier = jnp.arange(per_reader)[:, None] > jnp.arange(per_reader)[None, :]
    slot_rank = jnp.sum(((owners[:, None] == owners[None, :]) & earlier).astype(jnp.int32), 1)
    slot_range = jnp.arange(capacity, dtype=jnp.int32)
    local_index = block_ids % db_count
    owner_range = jnp.arange(dp_count, dtype=jnp.int32)
    slot_hit = (owners[:, None, None] == owner_range[None, :, None]) & (
        slot_rank[:, None, None] == slot_range[None, None, :]
    )
    request_table = jnp.sum(slot_hit.astype(jnp.int32) * local_index[:, None, None], 0)
    requested = lax.all_to_all(request_table, "dp", split_axis=0, concat_axis=0, tiled=True)
    outgoing = jnp.take(database, requested.reshape(-1), axis=0, mode="clip").reshape(
        dp_count, capacity, ret_len, col_count
    )
    arrived = lax.all_to_all(outgoing, "dp", split_axis=0, concat_axis=0, tiled=True)
    arrived_rows = arrived.reshape(dp_count * capacity, ret_len, col_count)
    arrived_slot = owners * capacity + slot_rank
    main_rows = per_reader - 2
    head_rows = pick(arrived_rows, arrived_slot[:main_rows])
    tail_rows = jnp.take(arrived_rows, arrived_slot[main_rows:], axis=0, mode="clip")
    main_parts = lax.all_gather(head_rows, "tensor", axis=0, tiled=False)
    w_key_parts = w_key.reshape(tensor_count, col_count, head_cols)
    w_value_parts = w_value.reshape(tensor_count, col_count, head_cols)
    w_both = lax.optimization_barrier(jnp.concatenate([w_key_parts, w_value_parts], axis=2))
    both_rows = jnp.einsum(
        "snkf,sfc->nkc", main_parts, w_both, preferred_element_type=jnp.float32
    ).astype(jnp.bfloat16)
    key_rows = both_rows[..., :head_cols].reshape(main_rows * ret_len, head_cols)
    value_rows = both_rows[..., head_cols:].reshape(main_rows * ret_len, head_cols)
    main_groups = main_rows // 2
    main_live = attend(
        query_rows[: main_groups * group_len], key_rows, value_rows, heads_local, group_len, main_groups
    )
    last_live = last_token(
        query_rows[main_groups * group_len], tail_rows, w_key, w_value, heads_local
    )
    live = jnp.concatenate([main_live, last_live[None]], 0)
    live_rows = live.shape[0]
    partial_out = jnp.einsum(
        "rc,csf->srf",
        live,
        w_out.reshape(head_cols, tensor_count, -1),
        preferred_element_type=jnp.float32,
    ).astype(jnp.bfloat16)
    spread = lax.all_to_all(partial_out, "tensor", split_axis=0, concat_axis=0, tiled=True)
    summed = jnp.sum(spread.astype(jnp.float32), axis=0).astype(jnp.bfloat16)
    return jnp.concatenate([jnp.zeros((group_len - 1, summed.shape[1]), jnp.bfloat16), summed], 0)


def solution(mesh):
    placed = (
        P("dp", "tensor"),
        P("dp", None),
        P("dp", None, "tensor"),
        P(None, "tensor"),
        P(None, "tensor"),
        P(None, "tensor"),
        P("tensor", None),
    )
    return jax.shard_map(
        shards, mesh=mesh, in_specs=placed, out_specs=P("dp", "tensor"), check_vma=False
    )
```

```python
import jax
import jax.numpy as jnp
from jax import lax
from jax.sharding import PartitionSpec as P

HD = 128


def attend(query_live, key_rows, value_rows, heads_count, group_len, groups):
    live_count, width = query_live.shape
    head_size = width // heads_count
    shifted = jnp.concatenate(
        [query_live, jnp.zeros((groups * group_len - live_count, width), jnp.bfloat16)], 0
    )
    shifted = shifted.reshape(groups, group_len, heads_count, head_size)
    key_block = key_rows.reshape(groups, -1, heads_count, head_size)
    value_block = value_rows.reshape(groups, -1, heads_count, head_size)
    scores = jnp.einsum(
        "cqhd,ckhd->chqk", shifted, key_block, preferred_element_type=jnp.float32
    ) / jnp.sqrt(jnp.float32(head_size))
    top_score = jnp.max(scores, axis=-1, keepdims=True)
    weights_raw = jnp.exp(scores - top_score)
    soft = (weights_raw / jnp.sum(weights_raw, axis=-1, keepdims=True)).astype(jnp.bfloat16)
    blended = jnp.einsum(
        "chqk,ckhd->cqhd", soft, value_block, preferred_element_type=jnp.float32
    ).astype(jnp.bfloat16)
    return blended.reshape(groups * group_len, width)[:live_count]


def last_token(query_row, tail_rows, w_key, w_value, heads_count):
    tensor_count = lax.axis_size("tensor")
    col_count = tail_rows.shape[-1]
    tail = tail_rows.reshape(-1, col_count)
    features = w_key.shape[0]
    head_size = query_row.shape[0] // heads_count
    exact = lax.Precision.HIGHEST
    spread_query = jnp.einsum(
        "fhd,hd->hf",
        w_key.reshape(features, heads_count, head_size),
        query_row.reshape(heads_count, head_size),
        preferred_element_type=jnp.float32,
    )
    own_query = lax.all_to_all(
        spread_query.reshape(heads_count, tensor_count, col_count),
        "tensor",
        split_axis=1,
        concat_axis=0,
        tiled=True,
    ).reshape(-1, col_count)
    partial_scores = jnp.einsum(
        "hf,kf->hk", own_query, tail, precision=exact, preferred_element_type=jnp.float32
    )
    all_scores = lax.all_to_all(
        jnp.broadcast_to(partial_scores[None], (tensor_count,) + partial_scores.shape),
        "tensor",
        split_axis=0,
        concat_axis=0,
        tiled=True,
    )
    scores = jnp.sum(all_scores, axis=0) / jnp.sqrt(jnp.float32(head_size))
    top_score = jnp.max(scores, axis=-1, keepdims=True)
    weights_raw = jnp.exp(scores - top_score)
    soft = (weights_raw / jnp.sum(weights_raw, axis=-1, keepdims=True)).astype(jnp.bfloat16)
    mixed_rows = jnp.einsum("hk,kf->hf", soft, tail, preferred_element_type=jnp.float32)
    own_rows = lax.all_to_all(
        mixed_rows.reshape(tensor_count, heads_count, col_count),
        "tensor",
        split_axis=0,
        concat_axis=0,
        tiled=True,
    )
    own_rows = jnp.transpose(own_rows, (1, 0, 2)).reshape(heads_count, features)
    context = jnp.einsum(
        "hf,fhd->hd",
        own_rows,
        w_value.reshape(features, heads_count, head_size),
        precision=exact,
        preferred_element_type=jnp.float32,
    )
    return context.astype(jnp.bfloat16).reshape(-1)


def shards(hidden, neighbour_ids, database, w_query, w_key, w_value, w_out):
    dp_count = lax.axis_size("dp")
    tok_rows = hidden.shape[0]
    group_count = neighbour_ids.shape[0]
    per_reader = group_count * neighbour_ids.shape[1]
    capacity = per_reader // 2
    db_count = database.shape[0]
    ret_len = database.shape[1]
    col_count = database.shape[2]
    head_cols = w_query.shape[1]
    heads_local = head_cols // HD
    tensor_count = lax.axis_size("tensor")
    group_len = tok_rows // group_count
    hidden_parts = lax.all_gather(hidden, "tensor", axis=0, tiled=False)
    query_sum = jnp.einsum(
        "srf,sfc->rc",
        hidden_parts[:, group_len - 1 :],
        w_query.reshape(tensor_count, -1, head_cols),
        preferred_element_type=jnp.float32,
    )
    query_rows = query_sum.astype(jnp.bfloat16)
    block_ids = neighbour_ids.reshape(per_reader)
    owners = block_ids // db_count
    earlier = jnp.arange(per_reader)[:, None] > jnp.arange(per_reader)[None, :]
    slot_rank = jnp.sum(((owners[:, None] == owners[None, :]) & earlier).astype(jnp.int32), 1)
    slot_range = jnp.arange(capacity, dtype=jnp.int32)
    local_index = block_ids % db_count
    owner_range = jnp.arange(dp_count, dtype=jnp.int32)
    slot_hit = (owners[:, None, None] == owner_range[None, :, None]) & (
        slot_rank[:, None, None] == slot_range[None, None, :]
    )
    request_table = jnp.sum(slot_hit.astype(jnp.int32) * local_index[:, None, None], 0)
    requested = lax.all_to_all(request_table, "dp", split_axis=0, concat_axis=0, tiled=True)
    outgoing = jnp.take(database, requested.reshape(-1), axis=0, mode="clip").reshape(
        dp_count, capacity, ret_len, col_count
    )
    arrived = lax.all_to_all(outgoing, "dp", split_axis=0, concat_axis=0, tiled=True)
    arrived_rows = arrived.reshape(dp_count * capacity, ret_len, col_count)
    arrived_slot = owners * capacity + slot_rank
    main_rows = per_reader - 2
    head_rows = jnp.take(arrived_rows, arrived_slot[:main_rows], axis=0, mode="clip")
    tail_rows = jnp.take(arrived_rows, arrived_slot[main_rows:], axis=0, mode="clip")
    main_parts = lax.all_gather(head_rows, "tensor", axis=0, tiled=False)
    w_key_parts = w_key.reshape(tensor_count, col_count, head_cols)
    w_value_parts = w_value.reshape(tensor_count, col_count, head_cols)
    w_both = lax.optimization_barrier(jnp.concatenate([w_key_parts, w_value_parts], axis=2))
    both_rows = jnp.einsum(
        "snkf,sfc->nkc", main_parts, w_both, preferred_element_type=jnp.float32
    ).astype(jnp.bfloat16)
    key_rows = both_rows[..., :head_cols].reshape(main_rows * ret_len, head_cols)
    value_rows = both_rows[..., head_cols:].reshape(main_rows * ret_len, head_cols)
    main_groups = main_rows // 2
    main_live = attend(
        query_rows[: main_groups * group_len], key_rows, value_rows, heads_local, group_len, main_groups
    )
    last_live = last_token(
        query_rows[main_groups * group_len], tail_rows, w_key, w_value, heads_local
    )
    live = jnp.concatenate([main_live, last_live[None]], 0)
    partial_out = jnp.einsum(
        "rc,csf->srf",
        live,
        w_out.reshape(head_cols, tensor_count, -1),
        preferred_element_type=jnp.float32,
    ).astype(jnp.bfloat16)
    spread = lax.all_to_all(partial_out, "tensor", split_axis=0, concat_axis=0, tiled=True)
    summed = jnp.sum(spread.astype(jnp.float32), axis=0).astype(jnp.bfloat16)
    return lax.dynamic_update_slice(
        jnp.zeros((tok_rows, summed.shape[1]), jnp.bfloat16), summed, (group_len - 1, 0)
    )


def solution(mesh):
    placed = (
        P("dp", "tensor"),
        P("dp", None),
        P("dp", None, "tensor"),
        P(None, "tensor"),
        P(None, "tensor"),
        P(None, "tensor"),
        P("tensor", None),
    )

    return jax.shard_map(
        shards, mesh=mesh, in_specs=placed, out_specs=P("dp", "tensor"), check_vma=False
    )
```

```python
import jax
import jax.numpy as jnp
from jax import lax
from jax.sharding import PartitionSpec as P

HD = 128


def attend(query_live, key_rows, value_rows, heads_count, group_len, groups):
    live_count, width = query_live.shape
    head_size = width // heads_count
    shifted = jnp.concatenate(
        [query_live, jnp.zeros((groups * group_len - live_count, width), jnp.bfloat16)], 0
    )
    shifted = shifted.reshape(groups, group_len, heads_count, head_size)
    key_block = key_rows.reshape(groups, -1, heads_count, head_size)
    value_block = value_rows.reshape(groups, -1, heads_count, head_size)
    scores = jnp.einsum(
        "cqhd,ckhd->chqk", shifted, key_block, preferred_element_type=jnp.float32
    ) / jnp.sqrt(jnp.float32(head_size))
    top_score = jnp.max(scores, axis=-1, keepdims=True)
    weights_raw = jnp.exp(scores - top_score)
    soft = (weights_raw / jnp.sum(weights_raw, axis=-1, keepdims=True)).astype(jnp.bfloat16)
    blended = jnp.einsum(
        "chqk,ckhd->cqhd", soft, value_block, preferred_element_type=jnp.float32
    ).astype(jnp.bfloat16)
    return blended.reshape(groups * group_len, width)[:live_count]


def last_token(query_row, tail_rows, w_key, w_value, heads_count):
    tensor_count = lax.axis_size("tensor")
    col_count = tail_rows.shape[-1]
    tail = tail_rows.reshape(-1, col_count)
    features = w_key.shape[0]
    head_size = query_row.shape[0] // heads_count
    exact = lax.Precision.HIGHEST
    spread_query = jnp.einsum(
        "fhd,hd->hf",
        w_key.reshape(features, heads_count, head_size),
        query_row.reshape(heads_count, head_size),
        preferred_element_type=jnp.float32,
    )
    own_query = lax.all_to_all(
        spread_query.reshape(heads_count, tensor_count, col_count),
        "tensor",
        split_axis=1,
        concat_axis=0,
        tiled=True,
    ).reshape(-1, col_count)
    partial_scores = jnp.einsum(
        "hf,kf->hk", own_query, tail, precision=exact, preferred_element_type=jnp.float32
    )
    all_scores = lax.all_to_all(
        jnp.broadcast_to(partial_scores[None], (tensor_count,) + partial_scores.shape),
        "tensor",
        split_axis=0,
        concat_axis=0,
        tiled=True,
    )
    scores = jnp.sum(all_scores, axis=0) / jnp.sqrt(jnp.float32(head_size))
    top_score = jnp.max(scores, axis=-1, keepdims=True)
    weights_raw = jnp.exp(scores - top_score)
    soft = (weights_raw / jnp.sum(weights_raw, axis=-1, keepdims=True)).astype(jnp.bfloat16)
    mixed_rows = jnp.einsum("hk,kf->hf", soft, tail, preferred_element_type=jnp.float32)
    own_rows = lax.all_to_all(
        mixed_rows.reshape(tensor_count, heads_count, col_count),
        "tensor",
        split_axis=0,
        concat_axis=0,
        tiled=True,
    )
    own_rows = jnp.transpose(own_rows, (1, 0, 2)).reshape(heads_count, features)
    context = jnp.einsum(
        "hf,fhd->hd",
        own_rows,
        w_value.reshape(features, heads_count, head_size),
        precision=exact,
        preferred_element_type=jnp.float32,
    )
    return context.astype(jnp.bfloat16).reshape(-1)


def pick(source, index):
    return jnp.stack(
        [lax.dynamic_index_in_dim(source, index[n], 0, keepdims=False) for n in range(index.shape[0])], 0
    )


def shards(hidden, neighbour_ids, database, w_query, w_key, w_value, w_out):
    dp_count = lax.axis_size("dp")
    tok_rows = hidden.shape[0]
    group_count = neighbour_ids.shape[0]
    per_reader = group_count * neighbour_ids.shape[1]
    capacity = per_reader // 2
    db_count = database.shape[0]
    ret_len = database.shape[1]
    col_count = database.shape[2]
    head_cols = w_query.shape[1]
    heads_local = head_cols // HD
    tensor_count = lax.axis_size("tensor")
    group_len = tok_rows // group_count
    hidden_parts = lax.all_gather(hidden, "tensor", axis=0, tiled=False)
    query_sum = jnp.einsum(
        "srf,sfc->rc",
        hidden_parts[:, group_len - 1 :],
        w_query.reshape(tensor_count, -1, head_cols),
        preferred_element_type=jnp.float32,
    )
    query_rows = query_sum.astype(jnp.bfloat16)
    block_ids = neighbour_ids.reshape(per_reader)
    owners = block_ids // db_count
    earlier = jnp.arange(per_reader)[:, None] > jnp.arange(per_reader)[None, :]
    slot_rank = jnp.sum(((owners[:, None] == owners[None, :]) & earlier).astype(jnp.int32), 1)
    slot_range = jnp.arange(capacity, dtype=jnp.int32)
    local_index = block_ids % db_count
    owner_range = jnp.arange(dp_count, dtype=jnp.int32)
    slot_hit = (owners[:, None, None] == owner_range[None, :, None]) & (
        slot_rank[:, None, None] == slot_range[None, None, :]
    )
    request_table = jnp.sum(slot_hit.astype(jnp.int32) * local_index[:, None, None], 0)
    requested = lax.all_to_all(request_table, "dp", split_axis=0, concat_axis=0, tiled=True)
    outgoing = jnp.take(database, requested.reshape(-1), axis=0, mode="clip").reshape(
        dp_count, capacity, ret_len, col_count
    )
    arrived = lax.all_to_all(outgoing, "dp", split_axis=0, concat_axis=0, tiled=True)
    arrived_rows = arrived.reshape(dp_count * capacity, ret_len, col_count)
    arrived_slot = owners * capacity + slot_rank
    main_rows = per_reader - 2
    head_rows = pick(arrived_rows, arrived_slot[:main_rows])
    tail_rows = jnp.take(arrived_rows, arrived_slot[main_rows:], axis=0, mode="clip")
    main_parts = lax.all_gather(head_rows, "tensor", axis=0, tiled=False)
    w_key_parts = w_key.reshape(tensor_count, col_count, head_cols)
    w_value_parts = w_value.reshape(tensor_count, col_count, head_cols)
    w_both = lax.optimization_barrier(jnp.concatenate([w_key_parts, w_value_parts], axis=2))
    both_rows = jnp.einsum(
        "snkf,sfc->nkc", main_parts, w_both, preferred_element_type=jnp.float32
    ).astype(jnp.bfloat16)
    key_rows = both_rows[..., :head_cols].reshape(main_rows * ret_len, head_cols)
    value_rows = both_rows[..., head_cols:].reshape(main_rows * ret_len, head_cols)
    main_groups = main_rows // 2
    main_live = attend(
        query_rows[: main_groups * group_len], key_rows, value_rows, heads_local, group_len, main_groups
    )
    last_live = last_token(
        query_rows[main_groups * group_len], tail_rows, w_key, w_value, heads_local
    )
    live = jnp.concatenate([main_live, last_live[None]], 0)
    live_rows = live.shape[0]
    partial_out = jnp.einsum(
        "rc,csf->srf",
        live,
        w_out.reshape(head_cols, tensor_count, -1),
        preferred_element_type=jnp.float32,
    ).astype(jnp.bfloat16)
    spread = lax.all_to_all(partial_out, "tensor", split_axis=0, concat_axis=0, tiled=True)
    summed = jnp.sum(spread.astype(jnp.float32), axis=0).astype(jnp.bfloat16)
    return jnp.concatenate([jnp.zeros((group_len - 1, summed.shape[1]), jnp.bfloat16), summed], 0)


def solution(mesh):
    placed = (
        P("dp", "tensor"),
        P("dp", None),
        P("dp", None, "tensor"),
        P(None, "tensor"),
        P(None, "tensor"),
        P(None, "tensor"),
        P("tensor", None),
    )
    return jax.shard_map(
        shards, mesh=mesh, in_specs=placed, out_specs=P("dp", "tensor"), check_vma=False
    )
```

```python
import jax
import jax.numpy as jnp
from jax import lax
from jax.sharding import PartitionSpec as P

HD = 128


def attend(query_live, key_rows, value_rows, heads_count, group_len, groups):
    live_count, width = query_live.shape
    head_size = width // heads_count
    shifted = jnp.concatenate(
        [query_live, jnp.zeros((groups * group_len - live_count, width), jnp.bfloat16)], 0
    )
    shifted = shifted.reshape(groups, group_len, heads_count, head_size)
    key_block = key_rows.reshape(groups, -1, heads_count, head_size)
    value_block = value_rows.reshape(groups, -1, heads_count, head_size)
    scores = jnp.einsum(
        "cqhd,ckhd->chqk", shifted, key_block, preferred_element_type=jnp.float32
    ) / jnp.sqrt(jnp.float32(head_size))
    top_score = jnp.max(scores, axis=-1, keepdims=True)
    weights_raw = jnp.exp(scores - top_score)
    soft = (weights_raw / jnp.sum(weights_raw, axis=-1, keepdims=True)).astype(jnp.bfloat16)
    blended = jnp.einsum(
        "chqk,ckhd->cqhd", soft, value_block, preferred_element_type=jnp.float32
    ).astype(jnp.bfloat16)
    return blended.reshape(groups * group_len, width)[:live_count]


def last_token(query_row, tail_rows, w_key, w_value, heads_count):
    tensor_count = lax.axis_size("tensor")
    col_count = tail_rows.shape[-1]
    tail = tail_rows.reshape(-1, col_count)
    features = w_key.shape[0]
    head_size = query_row.shape[0] // heads_count
    exact = lax.Precision.HIGHEST
    spread_query = jnp.einsum(
        "fhd,hd->hf",
        w_key.reshape(features, heads_count, head_size),
        query_row.reshape(heads_count, head_size),
        preferred_element_type=jnp.float32,
    )
    own_query = lax.all_to_all(
        spread_query.reshape(heads_count, tensor_count, col_count),
        "tensor",
        split_axis=1,
        concat_axis=0,
        tiled=True,
    ).reshape(-1, col_count)
    partial_scores = jnp.einsum(
        "hf,kf->hk", own_query, tail, precision=exact, preferred_element_type=jnp.float32
    )
    all_scores = lax.all_to_all(
        jnp.broadcast_to(partial_scores[None], (tensor_count,) + partial_scores.shape),
        "tensor",
        split_axis=0,
        concat_axis=0,
        tiled=True,
    )
    scores = jnp.sum(all_scores, axis=0) / jnp.sqrt(jnp.float32(head_size))
    top_score = jnp.max(scores, axis=-1, keepdims=True)
    weights_raw = jnp.exp(scores - top_score)
    soft = (weights_raw / jnp.sum(weights_raw, axis=-1, keepdims=True)).astype(jnp.bfloat16)
    mixed_rows = jnp.einsum("hk,kf->hf", soft, tail, preferred_element_type=jnp.float32)
    own_rows = lax.all_to_all(
        mixed_rows.reshape(tensor_count, heads_count, col_count),
        "tensor",
        split_axis=0,
        concat_axis=0,
        tiled=True,
    )
    own_rows = jnp.transpose(own_rows, (1, 0, 2)).reshape(heads_count, features)
    context = jnp.einsum(
        "hf,fhd->hd",
        own_rows,
        w_value.reshape(features, heads_count, head_size),
        precision=exact,
        preferred_element_type=jnp.float32,
    )
    return context.astype(jnp.bfloat16).reshape(-1)


def shards(hidden, neighbour_ids, database, w_query, w_key, w_value, w_out):
    dp_count = lax.axis_size("dp")
    tok_rows = hidden.shape[0]
    group_count = neighbour_ids.shape[0]
    per_reader = group_count * neighbour_ids.shape[1]
    capacity = per_reader // 2
    db_count = database.shape[0]
    ret_len = database.shape[1]
    col_count = database.shape[2]
    head_cols = w_query.shape[1]
    heads_local = head_cols // HD
    tensor_count = lax.axis_size("tensor")
    group_len = tok_rows // group_count
    hidden_parts = lax.all_gather(hidden, "tensor", axis=0, tiled=False)
    query_sum = jnp.einsum(
        "srf,sfc->rc",
        hidden_parts[:, group_len - 1 :],
        w_query.reshape(tensor_count, -1, head_cols),
        preferred_element_type=jnp.float32,
    )
    query_rows = query_sum.astype(jnp.bfloat16)
    block_ids = neighbour_ids.T.reshape(per_reader)
    owners = block_ids // db_count
    earlier = jnp.arange(per_reader)[:, None] > jnp.arange(per_reader)[None, :]
    slot_rank = jnp.sum(((owners[:, None] == owners[None, :]) & earlier).astype(jnp.int32), 1)
    slot_range = jnp.arange(capacity, dtype=jnp.int32)
    local_index = block_ids % db_count
    owner_range = jnp.arange(dp_count, dtype=jnp.int32)
    slot_hit = (owners[:, None, None] == owner_range[None, :, None]) & (
        slot_rank[:, None, None] == slot_range[None, None, :]
    )
    request_table = jnp.sum(slot_hit.astype(jnp.int32) * local_index[:, None, None], 0)
    requested = lax.all_to_all(request_table, "dp", split_axis=0, concat_axis=0, tiled=True)
    outgoing = jnp.take(database, requested.reshape(-1), axis=0, mode="clip").reshape(
        dp_count, capacity, ret_len, col_count
    )
    arrived = lax.all_to_all(outgoing, "dp", split_axis=0, concat_axis=0, tiled=True)
    arrived_rows = arrived.reshape(dp_count * capacity, ret_len, col_count)
    arrived_slot = (owners * capacity + slot_rank).reshape(-1, group_count).T.reshape(per_reader)
    main_rows = per_reader - 2
    head_rows = jnp.take(arrived_rows, arrived_slot[:main_rows], axis=0, mode="clip")
    tail_rows = jnp.take(arrived_rows, arrived_slot[main_rows:], axis=0, mode="clip")
    main_parts = lax.all_gather(head_rows, "tensor", axis=0, tiled=False)
    w_key_parts = w_key.reshape(tensor_count, col_count, head_cols)
    w_value_parts = w_value.reshape(tensor_count, col_count, head_cols)
    w_both = lax.optimization_barrier(jnp.concatenate([w_key_parts, w_value_parts], axis=2))
    both_rows = jnp.einsum(
        "snkf,sfc->nkc", main_parts, w_both, preferred_element_type=jnp.float32
    ).astype(jnp.bfloat16)
    key_rows = both_rows[..., :head_cols].reshape(main_rows * ret_len, head_cols)
    value_rows = both_rows[..., head_cols:].reshape(main_rows * ret_len, head_cols)
    main_groups = main_rows // 2
    main_live = attend(
        query_rows[: main_groups * group_len], key_rows, value_rows, heads_local, group_len, main_groups
    )
    last_live = last_token(
        query_rows[main_groups * group_len], tail_rows, w_key, w_value, heads_local
    )
    live = jnp.concatenate([main_live, last_live[None]], 0)
    live_rows = live.shape[0]
    partial_out = jnp.einsum(
        "rc,csf->srf",
        live,
        w_out.reshape(head_cols, tensor_count, -1),
        preferred_element_type=jnp.float32,
    ).astype(jnp.bfloat16)
    spread = lax.all_to_all(partial_out, "tensor", split_axis=0, concat_axis=0, tiled=True)
    summed = jnp.sum(spread.astype(jnp.float32), axis=0).astype(jnp.bfloat16)
    return jnp.concatenate([jnp.zeros((group_len - 1, summed.shape[1]), jnp.bfloat16), summed], 0)


def solution(mesh):
    placed = (
        P("dp", "tensor"),
        P("dp", None),
        P("dp", None, "tensor"),
        P(None, "tensor"),
        P(None, "tensor"),
        P(None, "tensor"),
        P("tensor", None),
    )
    return jax.shard_map(
        shards, mesh=mesh, in_specs=placed, out_specs=P("dp", "tensor"), check_vma=False
    )
```

```python
import jax
import jax.numpy as jnp
from jax import lax
from jax.sharding import PartitionSpec as P

HD = 128


def attend(query_live, key_rows, value_rows, heads_count, group_len, groups):
    live_count, width = query_live.shape
    head_size = width // heads_count
    shifted = jnp.concatenate(
        [query_live, jnp.zeros((groups * group_len - live_count, width), jnp.bfloat16)], 0
    )
    shifted = shifted.reshape(groups, group_len, heads_count, head_size)
    key_block = key_rows.reshape(groups, -1, heads_count, head_size)
    value_block = value_rows.reshape(groups, -1, heads_count, head_size)
    scores = jnp.einsum(
        "cqhd,ckhd->chqk", shifted, key_block, preferred_element_type=jnp.float32
    ) / jnp.sqrt(jnp.float32(head_size))
    top_score = jnp.max(scores, axis=-1, keepdims=True)
    weights_raw = jnp.exp(scores - top_score)
    soft = (weights_raw / jnp.sum(weights_raw, axis=-1, keepdims=True)).astype(jnp.bfloat16)
    blended = jnp.einsum(
        "chqk,ckhd->cqhd", soft, value_block, preferred_element_type=jnp.float32
    ).astype(jnp.bfloat16)
    return blended.reshape(groups * group_len, width)[:live_count]


def last_token(query_row, tail_rows, w_key, w_value, heads_count):
    tensor_count = lax.axis_size("tensor")
    col_count = tail_rows.shape[-1]
    tail = tail_rows.reshape(-1, col_count)
    features = w_key.shape[0]
    head_size = query_row.shape[0] // heads_count
    exact = lax.Precision.HIGHEST
    spread_query = jnp.einsum(
        "fhd,hd->hf",
        w_key.reshape(features, heads_count, head_size),
        query_row.reshape(heads_count, head_size),
        preferred_element_type=jnp.float32,
    )
    own_query = lax.all_to_all(
        spread_query.reshape(heads_count, tensor_count, col_count),
        "tensor",
        split_axis=1,
        concat_axis=0,
        tiled=True,
    ).reshape(-1, col_count)
    partial_scores = jnp.einsum(
        "hf,kf->hk", own_query, tail, precision=exact, preferred_element_type=jnp.float32
    )
    own_scores = lax.all_to_all(
        partial_scores.reshape(tensor_count, heads_count, -1),
        "tensor",
        split_axis=0,
        concat_axis=0,
        tiled=True,
    )
    scores = jnp.sum(own_scores, axis=0) / jnp.sqrt(jnp.float32(head_size))
    top_score = jnp.max(scores, axis=-1, keepdims=True)
    weights_raw = jnp.exp(scores - top_score)
    own_soft = (weights_raw / jnp.sum(weights_raw, axis=-1, keepdims=True)).astype(jnp.bfloat16)
    soft = lax.all_to_all(
        jnp.broadcast_to(own_soft[None], (tensor_count,) + own_soft.shape),
        "tensor",
        split_axis=0,
        concat_axis=0,
        tiled=True,
    ).reshape(tensor_count * heads_count, -1)
    mixed_rows = jnp.einsum("hk,kf->hf", soft, tail, preferred_element_type=jnp.float32)
    own_rows = lax.all_to_all(
        mixed_rows.reshape(tensor_count, heads_count, col_count),
        "tensor",
        split_axis=0,
        concat_axis=0,
        tiled=True,
    )
    own_rows = jnp.transpose(own_rows, (1, 0, 2)).reshape(heads_count, features)
    context = jnp.einsum(
        "hf,fhd->hd",
        own_rows,
        w_value.reshape(features, heads_count, head_size),
        precision=exact,
        preferred_element_type=jnp.float32,
    )
    return context.astype(jnp.bfloat16).reshape(-1)


def shards(hidden, neighbour_ids, database, w_query, w_key, w_value, w_out):
    dp_count = lax.axis_size("dp")
    tok_rows = hidden.shape[0]
    group_count = neighbour_ids.shape[0]
    per_reader = group_count * neighbour_ids.shape[1]
    capacity = per_reader // 2
    db_count = database.shape[0]
    ret_len = database.shape[1]
    col_count = database.shape[2]
    head_cols = w_query.shape[1]
    heads_local = head_cols // HD
    tensor_count = lax.axis_size("tensor")
    group_len = tok_rows // group_count
    hidden_parts = lax.all_gather(hidden, "tensor", axis=0, tiled=False)
    query_sum = jnp.einsum(
        "srf,sfc->rc",
        hidden_parts[:, group_len - 1 :],
        w_query.reshape(tensor_count, -1, head_cols),
        preferred_element_type=jnp.float32,
    )
    query_rows = query_sum.astype(jnp.bfloat16)
    block_ids = neighbour_ids.T.reshape(per_reader)
    owners = block_ids // db_count
    earlier = jnp.arange(per_reader)[:, None] > jnp.arange(per_reader)[None, :]
    slot_rank = jnp.sum(((owners[:, None] == owners[None, :]) & earlier).astype(jnp.int32), 1)
    slot_range = jnp.arange(capacity, dtype=jnp.int32)
    local_index = block_ids % db_count
    owner_range = jnp.arange(dp_count, dtype=jnp.int32)
    slot_hit = (owners[:, None, None] == owner_range[None, :, None]) & (
        slot_rank[:, None, None] == slot_range[None, None, :]
    )
    request_table = jnp.sum(slot_hit.astype(jnp.int32) * local_index[:, None, None], 0)
    requested = lax.all_to_all(request_table, "dp", split_axis=0, concat_axis=0, tiled=True)
    outgoing = jnp.take(database, requested.reshape(-1), axis=0, mode="clip").reshape(
        dp_count, capacity, ret_len, col_count
    )
    arrived = lax.all_to_all(outgoing, "dp", split_axis=0, concat_axis=0, tiled=True)
    arrived_rows = arrived.reshape(dp_count * capacity, ret_len, col_count)
    arrived_slot = (owners * capacity + slot_rank).reshape(-1, group_count).T.reshape(per_reader)
    main_rows = per_reader - 2
    head_rows = jnp.take(arrived_rows, arrived_slot[:main_rows], axis=0, mode="clip")
    tail_rows = jnp.take(arrived_rows, arrived_slot[main_rows:], axis=0, mode="clip")
    main_parts = lax.all_gather(head_rows, "tensor", axis=0, tiled=False)
    w_key_parts = w_key.reshape(tensor_count, col_count, head_cols)
    w_value_parts = w_value.reshape(tensor_count, col_count, head_cols)
    w_both = lax.optimization_barrier(jnp.concatenate([w_key_parts, w_value_parts], axis=2))
    both_rows = jnp.einsum(
        "snkf,sfc->nkc", main_parts, w_both, preferred_element_type=jnp.float32
    ).astype(jnp.bfloat16)
    key_rows = both_rows[..., :head_cols].reshape(main_rows * ret_len, head_cols)
    value_rows = both_rows[..., head_cols:].reshape(main_rows * ret_len, head_cols)
    main_groups = main_rows // 2
    main_live = attend(
        query_rows[: main_groups * group_len], key_rows, value_rows, heads_local, group_len, main_groups
    )
    last_live = last_token(
        query_rows[main_groups * group_len], tail_rows, w_key, w_value, heads_local
    )
    live = jnp.concatenate([main_live, last_live[None]], 0)
    partial_out = jnp.einsum(
        "rc,csf->srf",
        live,
        w_out.reshape(head_cols, tensor_count, -1),
        preferred_element_type=jnp.float32,
    ).astype(jnp.bfloat16)
    spread = lax.all_to_all(partial_out, "tensor", split_axis=0, concat_axis=0, tiled=True)
    summed = jnp.sum(spread.astype(jnp.float32), axis=0).astype(jnp.bfloat16)
    return lax.dynamic_update_slice(
        jnp.zeros((tok_rows, summed.shape[1]), jnp.bfloat16), summed, (group_len - 1, 0)
    )


def solution(mesh):
    placed = (
        P("dp", "tensor"),
        P("dp", None),
        P("dp", None, "tensor"),
        P(None, "tensor"),
        P(None, "tensor"),
        P(None, "tensor"),
        P("tensor", None),
    )

    return jax.shard_map(
        shards, mesh=mesh, in_specs=placed, out_specs=P("dp", "tensor"), check_vma=False
    )
```
